256 devices in a mesh: seq: 16 (over x, z_lo, core), hid: 16 (over z_hi, y).
Axes of the slice: x: 4, y: 4, z: 8 (z_hi: 4, z_lo: 2; z = z_hi * 2 + z_lo), core: 2. Of those that a mesh axis runs over, the one named last changes fastest.
Arguments:
- stream: bfloat16 [8192, 2048], P('seq'), may hold values from -5 to 5
- queries: bfloat16 [8192, 16, 128], P('seq', 'hid'), may hold values from -150 to 150
- key_rows: bfloat16 [8192, 16, 128], P('seq', 'hid'), may hold values from -5 to 5
- value_rows: bfloat16 [8192, 16, 128], P('seq', 'hid'), may hold values from -5 to 5
- segment_ids: int32 [8192], replicated, may hold values from 0 to 3, never falling along the last dimension, each value on 1 to 4096 neighbouring positions
- out_proj: bfloat16 [16, 128, 2048], P('hid'), may hold values from -0.125 to 0.125
- norm_gain: float32 [2048], replicated, may hold values from 0.1 to 1.9
- expert_ids: int32 [8192, 6], P('seq'), may hold values from 0 to 63, all different within a row; in each aligned block of 512 rows (0 to 511, 512 to 1023, ...) at most 64 rows name the same one
- route_gates: float32 [8192, 6], P('seq'), may hold values from 0.05 to 0.4
- gate_proj: bfloat16 [90112, 2048], P(('seq', 'hid')), may hold values from -0.125 to 0.125
- up_proj: bfloat16 [90112, 2048], P(('seq', 'hid')), may hold values from -0.125 to 0.125
- down_proj: bfloat16 [90112, 2048], P(('seq', 'hid')), may hold values from -0.15625 to 0.15625
- shared_gate: bfloat16 [2816, 2048], P('hid'), may hold values from -0.125 to 0.125
- shared_up: bfloat16 [2816, 2048], P('hid'), may hold values from -0.125 to 0.125
- shared_down: bfloat16 [2816, 2048], P('hid'), may hold values from -0.109375 to 0.109375
Outputs:
- layer_out: bfloat16 [8192, 2048], P('seq', 'hid')
The draws below stay inside these ranges and needn't reach their ends.
Inputs may be any that keep to these rules, and one draw needn't show every extreme that they name: `segment_ids`: segment numbers never fall along the tokens; every segment has at most 4096 tokens and one has exactly 4096. `expert_ids`: the 6 experts of a token differ; among the 512 tokens of one index of seq no expert is named by more than 64 tokens, a bound that some block reaches of them.
All inputs are finite; a program needn't handle non-finite values.
Results may differ from the reference program's by a relative error of at most 0.019.
Values may be sent and summed in bfloat16 or wider, within the bound.
No kernel may reach another device: no remote copies, remote signals or barrier semaphores. Data moves between devices by JAX's collectives and lax.ppermute only.
A program may use at most 128 MiB of HBM per device.

```python
import math
import jax
import jax.numpy as jnp
import numpy as np
from jax import lax

D = 2048
HEADS = 16
HEAD_DIM = 128
EXPERTS = 64
FF = 1408
SHARED_FF = 2816
TOP = 6
TOK_SEQ = 512
SEGS = 4
TOKENS = 8192
LONGEST = 4096
CAP = 64
FF_PARTS = 4
N_SEQ = 16
N_HID = 16


def drawn_rows(key):
    base_key = jax.random.fold_in(key, 4099)
    key_base = jnp.clip(jax.random.normal(jax.random.fold_in(base_key, 3), (TOKENS, HEADS, HEAD_DIM), jnp.float32), -5.0, 5.0)
    return key_base


def draw_key_rows(key, part):
    key_base = drawn_rows(key)
    return key_base.astype(jnp.bfloat16)


def draw_queries(key, part):
    query_noise = jnp.clip(jax.random.normal(jax.random.fold_in(key, 7001), (TOKENS, HEADS, HEAD_DIM), jnp.float32), -4.0, 4.0) * 1.5
    return query_noise.astype(jnp.bfloat16)


def block_levels(own_key, dims, shards, least, high):
    gain = 1.0
    for axis_at, parts in shards:
        heights = jax.random.uniform(jax.random.fold_in(jax.random.fold_in(own_key, 6), axis_at), (parts,), jnp.float32, least / len(shards), high / len(shards))
        gain = gain * jnp.repeat(jnp.exp(heights), dims[axis_at] // parts).reshape((-1,) + (1,) * (len(dims) - 1 - axis_at))
    return gain


def profile(amount, total, reach, lean):
    portions = [(1 << 20) // math.isqrt(grade ** lean) + 1 for grade in range(2, amount + 1)]
    surplus, counts = total - reach - (amount - 1), [1] * (amount - 1)
    while surplus > 0:
        movable = [i for i in range(amount - 1) if counts[i] < reach]
        pool, budget = sum([portions[i] for i in movable]), surplus
        for i in movable:
            addition = min(reach - counts[i], max(1, budget * portions[i] // pool), surplus)
            counts[i] = counts[i] + addition
            surplus = surplus - addition
    return np.array([reach] + counts)


def uneven_parts(rng, amount, total, reach, lean):
    if amount == 2:
        one = jax.random.randint(rng, (), max(1, total - reach), min(reach, total - 1) + 1)
        return jnp.stack([one, total - one])
    sizes = jnp.asarray(profile(amount, total, reach, lean), jnp.int32)
    couples = (amount - 1) // 2
    donor, sink = sizes[1:1 + 2 * couples:2], sizes[2:2 + 2 * couples:2]
    slack = jnp.minimum(donor - 1, reach - sink)
    moved = jax.random.randint(jax.random.fold_in(rng, 1), (couples,), 0, 1 << 20) % (slack + 1)
    sizes = sizes.at[1:1 + 2 * couples:2].set(donor - moved).at[2:2 + 2 * couples:2].set(sink + moved)
    return sizes[jax.random.permutation(jax.random.fold_in(rng, 2), amount)]


def routed_block(rng, own, number, rows, number_of, top, most, slope):
    ranking = jax.random.permutation(rng, number_of)
    crowded, common = load_shares(number_of, rows * top, most, slope, True), load_shares(number_of, rows * top, most, slope, False)
    places = jnp.arange(number_of)

    def named(tallies, rotation):
        used = int((tallies > 0).sum())
        fixed = max(1, used // 4)
        shifted = fixed + (places - fixed + rotation * (used - fixed)) % max(1, number_of - fixed)
        return jnp.zeros((number_of,), jnp.int32).at[ranking[jnp.where(places < fixed, places, shifted)]].set(jnp.asarray(tallies, jnp.int32))

    tallies = jnp.where(number % 4 == 0, named(crowded, number // 4), named(common, number - number // 4 - 1))
    mixed = jax.random.permutation(jax.random.fold_in(own, 3), number_of)
    source_of, taker = mixed[0:number_of // 2 * 2:2], mixed[1:number_of // 2 * 2:2]
    slack = jnp.minimum(tallies[source_of] - 1, most - tallies[taker]) // 2
    slack = jnp.where((source_of == ranking[0]) | (taker == ranking[0]) | (tallies[taker] == 0), 0, jnp.maximum(slack, 0))
    shifted = jax.random.randint(jax.random.fold_in(own, 4), (number_of // 2,), 0, 1 << 20) % (slack + 1)
    tallies = tallies.at[source_of].add(-shifted).at[taker].add(shifted)
    members = jnp.searchsorted(jnp.cumsum(tallies), jnp.arange(rows * top), side="right").astype(jnp.int32)
    grid = members.reshape(top, rows).T
    grid = grid[jax.random.permutation(jax.random.fold_in(own, 1), rows)]
    rotation = jax.random.randint(jax.random.fold_in(own, 2), (rows, 1), 0, top)
    return jnp.take_along_axis(grid, (jnp.arange(top)[None, :] + rotation) % top, axis=1)


def load_shares(number_of, total, bound, slope, full):
    weights = [(1 << 20) // math.isqrt(rank ** slope) + 1 for rank in range(1, number_of + 1)]
    largest = bound if full else min(bound, max(-(-total // number_of), total * weights[0] // sum(weights)))
    least = 1 if total - largest >= number_of - 1 else 0
    counts, rest = [largest] + [least] * (number_of - 1), total - largest - least * (number_of - 1)
    while rest > 0:
        free = [i for i in range(1, number_of) if counts[i] < largest] or [i for i in range(1, number_of) if counts[i] < bound]
        whole, remaining = sum([weights[i] for i in free]), rest
        for i in free:
            more = min(bound - counts[i], max(1, remaining * weights[i] // whole), rest)
            counts[i] = counts[i] + more
            rest = rest - more
    return np.array(counts)


def bell_draw(stream_key, dims, deviation, most, cuts=(), kind=jnp.bfloat16):
    entries = jax.random.normal(stream_key, dims, jnp.float32) * deviation
    if len(cuts) > 0:
        entries = block_levels(stream_key, dims, cuts, -0.22, 0.18) * entries
    return jnp.clip(entries, min=-most, max=most).astype(kind)


def setup_inputs(seed: int = 0) -> dict:
    keys = jax.random.split(jax.random.key(seed), 16)
    stream = bell_draw(keys[0], (TOKENS, D), 1.0, 5.0, ((0, 16),))
    queries = draw_queries(jax.random.fold_in(keys[15], 71), 0)
    key_rows = draw_key_rows(jax.random.fold_in(keys[15], 71), 0)
    value_rows = bell_draw(keys[3], (TOKENS, HEADS, HEAD_DIM), 1.0, 5.0, ((0, 16), (1, 16)))
    segment_ids = jnp.searchsorted(jnp.cumsum(uneven_parts(keys[4], SEGS, TOKENS, LONGEST, 2)), jnp.arange(TOKENS), side="right").astype(jnp.int32)
    out_proj = bell_draw(keys[5], (HEADS, HEAD_DIM, D), (HEADS * HEAD_DIM) ** -0.5, 0.125, ((0, 16),))
    norm_gain = jnp.clip(1.0 + 0.18 * jax.random.normal(keys[6], (D,), jnp.float32), 0.1, 1.9)
    expert_ids_keys = jax.random.split(jax.random.fold_in(keys[7], 1), TOKENS // TOK_SEQ)
    expert_ids_turns = jax.random.permutation(jax.random.fold_in(keys[7], 3), TOKENS // TOK_SEQ)
    expert_ids = jax.vmap(lambda own, number: routed_block(jax.random.fold_in(keys[7], 2), own, number, TOK_SEQ, EXPERTS, TOP, CAP, 2))(expert_ids_keys, expert_ids_turns).reshape((TOKENS, TOP))
    route_gates = jnp.clip(0.05 + 0.35 * jax.random.uniform(keys[8], (TOKENS, TOP), jnp.float32) ** block_levels(keys[8], (TOKENS, TOP), ((0, 16),), -0.2, 0.2), 0.05, 0.4)
    gate_proj = bell_draw(keys[9], (EXPERTS * FF, D), D ** -0.5, 0.125, ((0, 256),))
    up_proj = bell_draw(keys[10], (EXPERTS * FF, D), D ** -0.5, 0.125, ((0, 256),))
    down_proj = bell_draw(keys[11], (EXPERTS * FF, D), FF ** -0.5, 0.15625, ((0, 256),))
    shared_gate = bell_draw(keys[12], (SHARED_FF, D), D ** -0.5, 0.125, ((0, 16),))
    shared_up = bell_draw(keys[13], (SHARED_FF, D), D ** -0.5, 0.125, ((0, 16),))
    shared_down = bell_draw(keys[14], (SHARED_FF, D), SHARED_FF ** -0.5, 0.109375, ((0, 16),))
    return {"stream": stream, "queries": queries, "key_rows": key_rows, "value_rows": value_rows, "segment_ids": segment_ids, "out_proj": out_proj, "norm_gain": norm_gain, "expert_ids": expert_ids, "route_gates": route_gates, "gate_proj": gate_proj, "up_proj": up_proj, "down_proj": down_proj, "shared_gate": shared_gate, "shared_up": shared_up, "shared_down": shared_down}


def grouped_down(acts, downs, group_total):
    row_count = acts.shape[0]
    group_width = acts.shape[1] // group_total
    act_groups = acts.reshape(row_count, group_total, group_width).transpose(1, 0, 2)
    down_groups = downs.reshape(group_total, group_width, downs.shape[1])

    def add_group(running, group_pair):
        part_out = jnp.dot(group_pair[0], group_pair[1], preferred_element_type=jnp.float32).astype(jnp.bfloat16)
        part_out = lax.optimization_barrier(part_out)
        return (running + part_out.astype(jnp.float32), None)
    running, ignored = lax.scan(add_group, jnp.zeros((row_count, downs.shape[1]), jnp.float32), (act_groups, down_groups))
    return running

def reference(stream, queries, key_rows, value_rows, segment_ids, out_proj, norm_gain, expert_ids, route_gates, gate_proj, up_proj, down_proj, shared_gate, shared_up, shared_down):
    positions = jnp.arange(TOKENS, dtype=jnp.int32)
    allowed = (segment_ids[:, None] == segment_ids[None, :]) & (positions[None, :] <= positions[:, None])
    inv_root = HEAD_DIM ** (-0.5)

    def attend_head(head_rows):
        query_head, key_head, value_head = head_rows
        scores = jnp.dot(query_head, key_head.T, preferred_element_type=jnp.float32) * inv_root
        scores = jnp.where(allowed, scores, -1e+30)
        row_top = lax.optimization_barrier(jnp.max(scores, axis=1, keepdims=True))
        weights = jnp.where(allowed, jnp.exp(scores - row_top), 0.0)
        totals = lax.optimization_barrier(jnp.sum(weights, axis=1, keepdims=True))
        probs = weights.astype(jnp.bfloat16)
        attended = jnp.dot(probs, value_head, preferred_element_type=jnp.float32) / totals
        return attended.astype(jnp.bfloat16)
    per_head = lax.map(attend_head, (queries.transpose(1, 0, 2), key_rows.transpose(1, 0, 2), value_rows.transpose(1, 0, 2)))
    attended = per_head.transpose(1, 0, 2).reshape(TOKENS, HEADS * HEAD_DIM)
    mixed = stream.astype(jnp.float32) + jnp.dot(attended, out_proj.reshape(HEADS * HEAD_DIM, D), preferred_element_type=jnp.float32)
    mean_square = lax.optimization_barrier(jnp.mean(mixed * mixed, axis=1, keepdims=True))
    normed = (mixed * lax.rsqrt(mean_square + 1e-06) * norm_gain).astype(jnp.bfloat16)
    shared_gate_val = jnp.dot(normed, shared_gate.T, preferred_element_type=jnp.float32)
    shared_up_val = jnp.dot(normed, shared_up.T, preferred_element_type=jnp.float32)
    shared_act = (jax.nn.silu(shared_gate_val) * shared_up_val).astype(jnp.bfloat16)
    shared_out = grouped_down(shared_act, shared_down, N_HID)
    flat_ids = expert_ids.reshape(N_SEQ, TOK_SEQ * TOP)
    onehot = (flat_ids[:, :, None] == jnp.arange(EXPERTS, dtype=jnp.int32)[None, None, :]).astype(jnp.int32)
    slot_rank = lax.optimization_barrier(jnp.sum((jnp.cumsum(onehot, axis=1) - 1) * onehot, axis=2)).astype(jnp.int32)
    block_index = jnp.arange(N_SEQ, dtype=jnp.int32)[:, None]
    slot_index = (flat_ids * (N_SEQ * CAP) + block_index * CAP + slot_rank).reshape(-1).astype(jnp.int32)
    expert_input = jnp.zeros((EXPERTS * N_SEQ * CAP, D), jnp.bfloat16).at[slot_index].set(jnp.repeat(normed, TOP, axis=0))
    expert_input = expert_input.reshape(EXPERTS, N_SEQ * CAP, D)

    def run_expert(expert_parts):
        rows_in, gate_one, up_one, down_one = expert_parts
        gate_val = jnp.dot(rows_in, gate_one.T, preferred_element_type=jnp.float32)
        up_val = jnp.dot(rows_in, up_one.T, preferred_element_type=jnp.float32)
        expert_act = (jax.nn.silu(gate_val) * up_val).astype(jnp.bfloat16)
        return grouped_down(expert_act, down_one, FF_PARTS).astype(jnp.bfloat16)
    expert_out = lax.map(run_expert, (expert_input, gate_proj.reshape(EXPERTS, FF, D), up_proj.reshape(EXPERTS, FF, D), down_proj.reshape(EXPERTS, FF, D)))
    picked = expert_out.reshape(EXPERTS * N_SEQ * CAP, D)[slot_index].reshape(TOKENS, TOP, D).astype(jnp.float32)
    routed = lax.optimization_barrier(jnp.sum(route_gates[:, :, None] * picked, axis=1))
    return (mixed + shared_out + routed).astype(jnp.bfloat16)
```

```python
import jax
import jax.numpy as jnp
from jax import lax
from jax.sharding import PartitionSpec as P

EXPERTS = 64
FF = 1408
TOP = 6
CAP = 64


def seq_gather(rows, seq_count):
    spread = jnp.broadcast_to(rows[None], (seq_count,) + rows.shape)
    got = lax.all_to_all(spread, "seq", split_axis=0, concat_axis=0, tiled=True)
    return got.reshape((seq_count * rows.shape[0],) + rows.shape[1:])


def hid_scatter_sum(part, hid_count):
    rows, width = part.shape
    got = lax.all_to_all(
        part.reshape(rows, hid_count, width // hid_count),
        "hid",
        split_axis=1,
        concat_axis=1,
        tiled=True,
    )
    return jnp.sum(got.astype(jnp.float32), axis=1)


def on_device(
    stream,
    queries,
    key_rows,
    value_rows,
    segment_ids,
    out_proj,
    norm_gain,
    expert_ids,
    route_gates,
    gate_proj,
    up_proj,
    down_proj,
    shared_gate,
    shared_up,
    shared_down,
):
    tok_count = queries.shape[0]
    local_heads = queries.shape[1]
    head_width = queries.shape[2]
    width = stream.shape[1]
    inv_root = head_width ** (-0.5)
    seq_count = lax.axis_size("seq")
    hid_count = lax.axis_size("hid")
    hid_index = lax.axis_index("hid")
    query_first = lax.axis_index("seq") * tok_count
    query_seg = lax.dynamic_slice_in_dim(segment_ids, query_first, tok_count)
    query_pos = query_first + jnp.arange(tok_count, dtype=jnp.int32)
    run_max = jnp.full((tok_count, local_heads), -1e30, jnp.float32)
    key_part = seq_gather(key_rows, seq_count)
    value_part = seq_gather(value_rows, seq_count)
    row_count = key_part.shape[0]
    key_pos = jnp.arange(row_count, dtype=jnp.int32)
    scores = (
        jnp.einsum("qhd,khd->qhk", queries, key_part, preferred_element_type=jnp.float32) * inv_root
    )
    allowed = (query_seg[:, None] == segment_ids[None, :]) & (
        key_pos[None, :] <= query_pos[:, None]
    )
    scores = jnp.where(allowed[:, None, :], scores, -1e30)
    new_max = jnp.maximum(run_max, jnp.max(scores, axis=2))
    weights = jnp.where(allowed[:, None, :], jnp.exp(scores - new_max[:, :, None]), 0.0)
    new_sum = jnp.sum(weights, axis=2)
    probs = weights.astype(jnp.bfloat16)
    new_acc = jnp.einsum("qhk,khd->qhd", probs, value_part, preferred_element_type=jnp.float32)
    attended = (
        (new_acc / new_sum[:, :, None])
        .astype(jnp.bfloat16)
        .reshape(tok_count, local_heads * head_width)
    )
    out_flat = out_proj.reshape(local_heads * head_width, width)
    partial_mix = jnp.dot(attended, out_flat, preferred_element_type=jnp.float32)
    col_count = width // hid_count
    col_first = hid_index * col_count
    mixed_cols = lax.dynamic_slice_in_dim(stream, col_first, col_count, 1).astype(
        jnp.float32
    ) + hid_scatter_sum(partial_mix.astype(jnp.bfloat16), hid_count)
    square_part = jnp.sum(mixed_cols * mixed_cols, axis=1)
    square_all = lax.all_to_all(
        jnp.broadcast_to(square_part[None, :], (hid_count, tok_count)),
        "hid",
        split_axis=0,
        concat_axis=0,
        tiled=True,
    )
    mean_square = (jnp.sum(square_all, axis=0) / width)[:, None]
    gain_cols = lax.dynamic_slice_in_dim(norm_gain, col_first, col_count, 0)
    normed_cols = (mixed_cols * lax.rsqrt(mean_square + 1e-06) * gain_cols).astype(jnp.bfloat16)
    normed = lax.all_to_all(
        jnp.broadcast_to(normed_cols[:, None, :], (tok_count, hid_count, col_count)),
        "hid",
        split_axis=1,
        concat_axis=1,
        tiled=True,
    ).reshape(tok_count, width)
    shared_gate_val = jnp.einsum(
        "td,fd->tf", normed, shared_gate, preferred_element_type=jnp.float32
    )
    shared_up_val = jnp.einsum("td,fd->tf", normed, shared_up, preferred_element_type=jnp.float32)
    shared_act = (jax.nn.silu(shared_gate_val) * shared_up_val).astype(jnp.bfloat16)
    shared_part = jnp.dot(shared_act, shared_down, preferred_element_type=jnp.float32)
    shared_out = hid_scatter_sum(shared_part.astype(jnp.bfloat16), hid_count)
    unit_rows = gate_proj.shape[0]
    held_count = max(1, unit_rows // FF)
    held_units = unit_rows // held_count
    local_experts = EXPERTS // seq_count
    first_local = hid_index * unit_rows // FF
    flat_ids = expert_ids.reshape(-1)
    onehot = (flat_ids[:, None] == jnp.arange(EXPERTS, dtype=jnp.int32)[None, :]).astype(jnp.int32)
    slot_rank = jnp.sum((jnp.cumsum(onehot, axis=0) - 1) * onehot, axis=1)
    owner_group = flat_ids // local_experts
    local_expert = flat_ids % local_experts
    held_offset = local_expert - first_local
    is_held = (held_offset >= 0) & (held_offset < held_count)
    slot_total = seq_count * held_count * CAP
    send_index = jnp.where(
        is_held, (owner_group * held_count + held_offset) * CAP + slot_rank, slot_total
    )
    route_token = jnp.arange(tok_count * TOP, dtype=jnp.int32) // TOP
    slot_token = jnp.full((slot_total,), -1, jnp.int32).at[send_index].set(route_token, mode="drop")
    send_rows = jnp.where(
        (slot_token >= 0)[:, None], normed[jnp.maximum(slot_token, 0)], jnp.zeros((), jnp.bfloat16)
    )
    send_rows = send_rows.reshape(seq_count, held_count, CAP, width)
    received = lax.all_to_all(send_rows, "seq", split_axis=0, concat_axis=0, tiled=True)
    gate_local = gate_proj.reshape(held_count, held_units, width)
    up_local = up_proj.reshape(held_count, held_units, width)
    down_local = down_proj.reshape(held_count, held_units, hid_count, col_count)
    gate_val = jnp.einsum(
        "sicd,ifd->sicf", received, gate_local, preferred_element_type=jnp.float32
    )
    up_val = jnp.einsum("sicd,ifd->sicf", received, up_local, preferred_element_type=jnp.float32)
    expert_act = (jax.nn.silu(gate_val) * up_val).astype(jnp.bfloat16)
    down_part = jnp.einsum(
        "sicf,ifnx->niscx", expert_act, down_local, preferred_element_type=jnp.float32
    ).astype(jnp.bfloat16)
    down_part = down_part.reshape(hid_count, held_count, seq_count * CAP, col_count)
    peer_parts = lax.all_to_all(down_part, "hid", split_axis=0, concat_axis=0, tiled=True)
    part_count = hid_count * held_count // local_experts
    expert_out = jnp.sum(
        peer_parts.reshape(local_experts, part_count, seq_count * CAP, col_count).astype(
            jnp.float32
        ),
        axis=1,
    ).astype(jnp.bfloat16)
    returned = lax.all_to_all(
        expert_out.reshape(local_experts, seq_count, CAP, col_count),
        "seq",
        split_axis=1,
        concat_axis=1,
        tiled=True,
    ).reshape(-1, col_count)
    pick_index = local_expert * (seq_count * CAP) + owner_group * CAP + slot_rank
    picked = returned[pick_index].reshape(tok_count, TOP, col_count)
    routed_sum = jnp.einsum("tj,tjd->td", route_gates, picked.astype(jnp.float32))
    return (mixed_cols + shared_out + routed_sum).astype(jnp.bfloat16)


def solution(mesh):
    placed = (
        P("seq", None),
        P("seq", "hid", None),
        P("seq", "hid", None),
        P("seq", "hid", None),
        P(),
        P("hid", None, None),
        P(),
        P("seq", None),
        P("seq", None),
        P(("seq", "hid"), None),
        P(("seq", "hid"), None),
        P(("seq", "hid"), None),
        P("hid", None),
        P("hid", None),
        P("hid", None),
    )
    return jax.shard_map(
        on_device, mesh=mesh, in_specs=placed, out_specs=P("seq", "hid"), check_vma=False
    )
```

```python
import jax
import jax.numpy as jnp
from jax import lax
from jax.sharding import PartitionSpec as P

EXPERTS = 64
FF = 1408
TOP = 6
CAP = 64
LONGEST = 4096


def seq_gather(rows, seq_count):
    spread = jnp.broadcast_to(rows[None], (seq_count,) + rows.shape)
    got = lax.all_to_all(spread, "seq", split_axis=0, concat_axis=0, tiled=True)
    return got.reshape((seq_count * rows.shape[0],) + rows.shape[1:])


def hid_scatter_sum(part, hid_count):
    rows, width = part.shape
    got = lax.all_to_all(
        part.reshape(rows, hid_count, width // hid_count),
        "hid",
        split_axis=1,
        concat_axis=1,
        tiled=True,
    )
    return jnp.sum(got.astype(jnp.float32), axis=1)


def hid_permute_sum(part, hid_count, hid_index):
    rows, width = part.shape
    chunks = part.reshape(rows, hid_count, width // hid_count)
    total = lax.dynamic_index_in_dim(chunks, hid_index, 1, keepdims=False).astype(jnp.float32)
    for shift in range(1, hid_count):
        sent = lax.dynamic_index_in_dim(chunks, (hid_index + shift) % hid_count, 1, keepdims=False)
        pairs = [(i, (i + shift) % hid_count) for i in range(hid_count)]
        total = total + lax.ppermute(sent, "hid", pairs).astype(jnp.float32)
    return total


def on_device(
    stream,
    queries,
    key_rows,
    value_rows,
    segment_ids,
    out_proj,
    norm_gain,
    expert_ids,
    route_gates,
    gate_proj,
    up_proj,
    down_proj,
    shared_gate,
    shared_up,
    shared_down,
):
    tok_count = queries.shape[0]
    local_heads = queries.shape[1]
    head_width = queries.shape[2]
    width = stream.shape[1]
    inv_root = head_width ** (-0.5)
    seq_count = lax.axis_size("seq")
    hid_count = lax.axis_size("hid")
    hid_index = lax.axis_index("hid")
    query_first = lax.axis_index("seq") * tok_count
    query_seg = lax.dynamic_slice_in_dim(segment_ids, query_first, tok_count)
    query_pos = query_first + jnp.arange(tok_count, dtype=jnp.int32)
    run_max = jnp.full((tok_count, local_heads), -1e30, jnp.float32)
    window = min(seq_count, -(-LONGEST // tok_count) + 1)
    both = jnp.concatenate([key_rows, value_rows], axis=1)
    blocks = [both]
    for shift in range(1, window):
        pairs = [(i, i + shift) for i in range(seq_count - shift)]
        blocks.append(lax.ppermute(both, "seq", pairs))
    both_win = jnp.concatenate(blocks[::-1], axis=0)
    key_part = both_win[:, :local_heads]
    value_part = both_win[:, local_heads:]
    row_count = key_part.shape[0]
    key_first = query_first - (window - 1) * tok_count
    key_pos = key_first + jnp.arange(row_count, dtype=jnp.int32)
    seg_padded = jnp.concatenate(
        [jnp.full(((window - 1) * tok_count,), -1, jnp.int32), segment_ids]
    )
    key_seg = lax.dynamic_slice_in_dim(seg_padded, query_first, row_count)
    scores = (
        jnp.einsum("qhd,khd->qhk", queries, key_part, preferred_element_type=jnp.float32) * inv_root
    )
    allowed = (query_seg[:, None] == key_seg[None, :]) & (
        key_pos[None, :] <= query_pos[:, None]
    )
    scores = jnp.where(allowed[:, None, :], scores, -1e30)
    new_max = jnp.maximum(run_max, jnp.max(scores, axis=2))
    weights = jnp.where(allowed[:, None, :], jnp.exp(scores - new_max[:, :, None]), 0.0)
    new_sum = jnp.sum(weights, axis=2)
    probs = weights.astype(jnp.bfloat16)
    new_acc = jnp.einsum("qhk,khd->qhd", probs, value_part, preferred_element_type=jnp.float32)
    attended = (
        (new_acc / new_sum[:, :, None])
        .astype(jnp.bfloat16)
        .reshape(tok_count, local_heads * head_width)
    )
    out_flat = out_proj.reshape(local_heads * head_width, width)
    partial_mix = jnp.dot(attended, out_flat, preferred_element_type=jnp.float32)
    col_count = width // hid_count
    col_first = hid_index * col_count
    mixed_cols = lax.dynamic_slice_in_dim(stream, col_first, col_count, 1).astype(
        jnp.float32
    ) + hid_scatter_sum(partial_mix.astype(jnp.bfloat16), hid_count)
    mixed_all = lax.all_to_all(
        jnp.broadcast_to(
            mixed_cols.astype(jnp.bfloat16)[:, None, :], (tok_count, hid_count, col_count)
        ),
        "hid",
        split_axis=1,
        concat_axis=1,
        tiled=True,
    ).reshape(tok_count, width).astype(jnp.float32)
    mean_square = jnp.mean(mixed_all * mixed_all, axis=1, keepdims=True)
    normed = (mixed_all * lax.rsqrt(mean_square + 1e-06) * norm_gain).astype(jnp.bfloat16)
    shared_gate_val = jnp.einsum(
        "td,fd->tf", normed, shared_gate, preferred_element_type=jnp.float32
    )
    shared_up_val = jnp.einsum("td,fd->tf", normed, shared_up, preferred_element_type=jnp.float32)
    shared_act = (jax.nn.silu(shared_gate_val) * shared_up_val).astype(jnp.bfloat16)
    shared_part = jnp.dot(shared_act, shared_down, preferred_element_type=jnp.float32)
    shared_out = hid_scatter_sum(shared_part.astype(jnp.bfloat16), hid_count)
    unit_rows = gate_proj.shape[0]
    held_count = max(1, unit_rows // FF)
    held_units = unit_rows // held_count
    local_experts = EXPERTS // seq_count
    first_local = hid_index * unit_rows // FF
    flat_ids = expert_ids.reshape(-1)
    onehot = (flat_ids[:, None] == jnp.arange(EXPERTS, dtype=jnp.int32)[None, :]).astype(jnp.int32)
    slot_rank = jnp.sum((jnp.cumsum(onehot, axis=0) - 1) * onehot, axis=1)
    owner_group = flat_ids // local_experts
    local_expert = flat_ids % local_experts
    held_offset = local_expert - first_local
    is_held = (held_offset >= 0) & (held_offset < held_count)
    slot_total = seq_count * held_count * CAP
    send_index = jnp.where(
        is_held, (owner_group * held_count + held_offset) * CAP + slot_rank, slot_total
    )
    route_token = jnp.arange(tok_count * TOP, dtype=jnp.int32) // TOP
    slot_token = jnp.full((slot_total,), -1, jnp.int32).at[send_index].set(route_token, mode="drop")
    send_rows = jnp.where(
        (slot_token >= 0)[:, None], normed[jnp.maximum(slot_token, 0)], jnp.zeros((), jnp.bfloat16)
    )
    send_rows = send_rows.reshape(seq_count, held_count, CAP, width)
    received = lax.all_to_all(send_rows, "seq", split_axis=0, concat_axis=0, tiled=True)
    gate_local = gate_proj.reshape(held_count, held_units, width)
    up_local = up_proj.reshape(held_count, held_units, width)
    down_local = down_proj.reshape(held_count, held_units, hid_count, col_count)
    gate_val = jnp.einsum(
        "sicd,ifd->sicf", received, gate_local, preferred_element_type=jnp.float32
    )
    up_val = jnp.einsum("sicd,ifd->sicf", received, up_local, preferred_element_type=jnp.float32)
    expert_act = (jax.nn.silu(gate_val) * up_val).astype(jnp.bfloat16)
    down_part = jnp.einsum(
        "sicf,ifnx->niscx", expert_act, down_local, preferred_element_type=jnp.float32
    ).astype(jnp.bfloat16)
    down_part = down_part.reshape(hid_count, held_count, seq_count * CAP, col_count)
    peer_parts = lax.all_to_all(down_part, "hid", split_axis=0, concat_axis=0, tiled=True)
    part_count = hid_count * held_count // local_experts
    expert_out = jnp.sum(
        peer_parts.reshape(local_experts, part_count, seq_count * CAP, col_count).astype(
            jnp.float32
        ),
        axis=1,
    ).astype(jnp.bfloat16)
    returned = lax.all_to_all(
        expert_out.reshape(local_experts, seq_count, CAP, col_count),
        "seq",
        split_axis=1,
        concat_axis=1,
        tiled=True,
    ).reshape(-1, col_count)
    pick_index = local_expert * (seq_count * CAP) + owner_group * CAP + slot_rank
    picked = returned[pick_index].reshape(tok_count, TOP, col_count)
    routed_sum = jnp.einsum("tj,tjd->td", route_gates, picked.astype(jnp.float32))
    return (mixed_cols + shared_out + routed_sum).astype(jnp.bfloat16)


def solution(mesh):
    placed = (
        P("seq", None),
        P("seq", "hid", None),
        P("seq", "hid", None),
        P("seq", "hid", None),
        P(),
        P("hid", None, None),
        P(),
        P("seq", None),
        P("seq", None),
        P(("seq", "hid"), None),
        P(("seq", "hid"), None),
        P(("seq", "hid"), None),
        P("hid", None),
        P("hid", None),
        P("hid", None),
    )
    return jax.shard_map(
        on_device, mesh=mesh, in_specs=placed, out_specs=P("seq", "hid"), check_vma=False
    )
```

```python
import jax
import jax.numpy as jnp
from jax import lax
from jax.sharding import PartitionSpec as P

EXPERTS = 64
FF = 1408
TOP = 6
CAP = 64
LONGEST = 4096


def seq_gather(rows, seq_count):
    spread = jnp.broadcast_to(rows[None], (seq_count,) + rows.shape)
    got = lax.all_to_all(spread, "seq", split_axis=0, concat_axis=0, tiled=True)
    return got.reshape((seq_count * rows.shape[0],) + rows.shape[1:])


def hid_scatter_sum(part, hid_count):
    rows, width = part.shape
    got = lax.all_to_all(
        part.reshape(rows, hid_count, width // hid_count),
        "hid",
        split_axis=1,
        concat_axis=1,
        tiled=True,
    )
    return jnp.sum(got.astype(jnp.float32), axis=1)


def hid_permute_sum(part, hid_count, hid_index):
    rows, width = part.shape
    chunks = part.reshape(rows, hid_count, width // hid_count)
    total = lax.dynamic_index_in_dim(chunks, hid_index, 1, keepdims=False).astype(jnp.float32)
    for shift in range(1, hid_count):
        sent = lax.dynamic_index_in_dim(chunks, (hid_index + shift) % hid_count, 1, keepdims=False)
        pairs = [(i, (i + shift) % hid_count) for i in range(hid_count)]
        total = total + lax.ppermute(sent, "hid", pairs).astype(jnp.float32)
    return total


def route_ranks(flat_ids):
    span = 64
    blocks = flat_ids.shape[0] // span
    onehot = (flat_ids[:, None] == jnp.arange(EXPERTS, dtype=jnp.int32)[None, :]).astype(
        jnp.bfloat16
    )
    onehot = onehot.reshape(blocks, span, EXPERTS)
    lower = jnp.arange(span)[:, None] >= jnp.arange(span)[None, :]
    within = jnp.einsum(
        "ij,bjk->bik", lower.astype(jnp.bfloat16), onehot, preferred_element_type=jnp.float32
    )
    earlier = jnp.arange(blocks)[:, None] > jnp.arange(blocks)[None, :]
    before = jnp.dot(
        earlier.astype(jnp.bfloat16),
        within[:, -1, :].astype(jnp.bfloat16),
        preferred_element_type=jnp.float32,
    )
    counts = within + before[:, None, :]
    ranks = jnp.sum(counts * onehot.astype(jnp.float32), axis=2) - 1.0
    return ranks.astype(jnp.int32).reshape(-1)


def on_device(
    stream,
    queries,
    key_rows,
    value_rows,
    segment_ids,
    out_proj,
    norm_gain,
    expert_ids,
    route_gates,
    gate_proj,
    up_proj,
    down_proj,
    shared_gate,
    shared_up,
    shared_down,
):
    tok_count = queries.shape[0]
    local_heads = queries.shape[1]
    head_width = queries.shape[2]
    width = stream.shape[1]
    inv_root = head_width ** (-0.5)
    seq_count = lax.axis_size("seq")
    hid_count = lax.axis_size("hid")
    hid_index = lax.axis_index("hid")
    query_first = lax.axis_index("seq") * tok_count
    query_seg = lax.dynamic_slice_in_dim(segment_ids, query_first, tok_count)
    query_pos = query_first + jnp.arange(tok_count, dtype=jnp.int32)
    run_max = jnp.full((tok_count, local_heads), -1e30, jnp.float32)
    window = min(seq_count, -(-LONGEST // tok_count) + 1)
    both = jnp.concatenate([key_rows, value_rows], axis=1)
    blocks = [both]
    for shift in range(1, window):
        pairs = [(i, i + shift) for i in range(seq_count - shift)]
        blocks.append(lax.ppermute(both, "seq", pairs))
    both_win = jnp.concatenate(blocks[::-1], axis=0)
    key_part = both_win[:, :local_heads]
    value_part = both_win[:, local_heads:]
    row_count = key_part.shape[0]
    key_first = query_first - (window - 1) * tok_count
    key_pos = key_first + jnp.arange(row_count, dtype=jnp.int32)
    seg_padded = jnp.concatenate(
        [jnp.full(((window - 1) * tok_count,), -1, jnp.int32), segment_ids]
    )
    key_seg = lax.dynamic_slice_in_dim(seg_padded, query_first, row_count)
    scores = (
        jnp.einsum("qhd,khd->qhk", queries, key_part, preferred_element_type=jnp.float32) * inv_root
    )
    allowed = (query_seg[:, None] == key_seg[None, :]) & (
        key_pos[None, :] <= query_pos[:, None]
    )
    scores = jnp.where(allowed[:, None, :], scores, -1e30)
    new_max = jnp.maximum(run_max, jnp.max(scores, axis=2))
    weights = jnp.where(allowed[:, None, :], jnp.exp(scores - new_max[:, :, None]), 0.0)
    new_sum = jnp.sum(weights, axis=2)
    probs = weights.astype(jnp.bfloat16)
    new_acc = jnp.einsum("qhk,khd->qhd", probs, value_part, preferred_element_type=jnp.float32)
    attended = (
        (new_acc / new_sum[:, :, None])
        .astype(jnp.bfloat16)
        .reshape(tok_count, local_heads * head_width)
    )
    out_flat = out_proj.reshape(local_heads * head_width, width)
    partial_mix = jnp.dot(attended, out_flat, preferred_element_type=jnp.float32)
    col_count = width // hid_count
    col_first = hid_index * col_count
    mixed_cols = lax.dynamic_slice_in_dim(stream, col_first, col_count, 1).astype(
        jnp.float32
    ) + hid_scatter_sum(partial_mix.astype(jnp.bfloat16), hid_count)
    mixed_all = lax.all_to_all(
        jnp.broadcast_to(
            mixed_cols.astype(jnp.bfloat16)[:, None, :], (tok_count, hid_count, col_count)
        ),
        "hid",
        split_axis=1,
        concat_axis=1,
        tiled=True,
    ).reshape(tok_count, width).astype(jnp.float32)
    mean_square = jnp.mean(mixed_all * mixed_all, axis=1, keepdims=True)
    normed = (mixed_all * lax.rsqrt(mean_square + 1e-06) * norm_gain).astype(jnp.bfloat16)
    shared_gate_val = jnp.einsum(
        "td,fd->tf", normed, shared_gate, preferred_element_type=jnp.float32
    )
    shared_up_val = jnp.einsum("td,fd->tf", normed, shared_up, preferred_element_type=jnp.float32)
    shared_act = (jax.nn.silu(shared_gate_val) * shared_up_val).astype(jnp.bfloat16)
    shared_part = jnp.dot(shared_act, shared_down, preferred_element_type=jnp.float32)
    shared_out = hid_scatter_sum(shared_part.astype(jnp.bfloat16), hid_count)
    unit_rows = gate_proj.shape[0]
    held_count = max(1, unit_rows // FF)
    held_units = unit_rows // held_count
    local_experts = EXPERTS // seq_count
    first_local = hid_index * unit_rows // FF
    flat_ids = expert_ids.reshape(-1)
    slot_rank = route_ranks(flat_ids)
    owner_group = flat_ids // local_experts
    local_expert = flat_ids % local_experts
    held_offset = local_expert - first_local
    is_held = (held_offset >= 0) & (held_offset < held_count)
    slot_total = seq_count * held_count * CAP
    send_index = jnp.where(
        is_held, (owner_group * held_count + held_offset) * CAP + slot_rank, slot_total
    )
    slot_ids = jnp.arange(slot_total, dtype=jnp.int32)
    picks = jnp.any(
        send_index.reshape(tok_count, TOP)[None, :, :] == slot_ids[:, None, None], axis=2
    ).astype(jnp.bfloat16)
    send_rows = jnp.dot(picks, normed, preferred_element_type=jnp.float32).astype(jnp.bfloat16)
    send_rows = send_rows.reshape(seq_count, held_count, CAP, width)
    received = lax.all_to_all(send_rows, "seq", split_axis=0, concat_axis=0, tiled=True)
    gate_local = gate_proj.reshape(held_count, held_units, width)
    up_local = up_proj.reshape(held_count, held_units, width)
    down_local = down_proj.reshape(held_count, held_units, hid_count, col_count)
    gate_val = jnp.einsum(
        "sicd,ifd->sicf", received, gate_local, preferred_element_type=jnp.float32
    )
    up_val = jnp.einsum("sicd,ifd->sicf", received, up_local, preferred_element_type=jnp.float32)
    expert_act = (jax.nn.silu(gate_val) * up_val).astype(jnp.bfloat16)
    down_part = jnp.einsum(
        "sicf,ifnx->niscx", expert_act, down_local, preferred_element_type=jnp.float32
    ).astype(jnp.bfloat16)
    down_part = down_part.reshape(hid_count, held_count, seq_count * CAP, col_count)
    peer_parts = lax.all_to_all(down_part, "hid", split_axis=0, concat_axis=0, tiled=True)
    part_count = hid_count * held_count // local_experts
    expert_out = jnp.sum(
        peer_parts.reshape(local_experts, part_count, seq_count * CAP, col_count).astype(
            jnp.float32
        ),
        axis=1,
    ).astype(jnp.bfloat16)
    returned = lax.all_to_all(
        expert_out.reshape(local_experts, seq_count, CAP, col_count),
        "seq",
        split_axis=1,
        concat_axis=1,
        tiled=True,
    ).reshape(-1, col_count)
    pick_index = local_expert * (seq_count * CAP) + owner_group * CAP + slot_rank
    picked = returned[pick_index].reshape(tok_count, TOP, col_count)
    routed_sum = jnp.einsum("tj,tjd->td", route_gates, picked.astype(jnp.float32))
    return (mixed_cols + shared_out + routed_sum).astype(jnp.bfloat16)


def solution(mesh):
    placed = (
        P("seq", None),
        P("seq", "hid", None),
        P("seq", "hid", None),
        P("seq", "hid", None),
        P(),
        P("hid", None, None),
        P(),
        P("seq", None),
        P("seq", None),
        P(("seq", "hid"), None),
        P(("seq", "hid"), None),
        P(("seq", "hid"), None),
        P("hid", None),
        P("hid", None),
        P("hid", None),
    )
    return jax.shard_map(
        on_device, mesh=mesh, in_specs=placed, out_specs=P("seq", "hid"), check_vma=False
    )
```

```python
import jax
import jax.numpy as jnp
from jax import lax
from jax.sharding import Mesh, PartitionSpec as P

EXPERTS = 64
FF = 1408
TOP = 6
CAP = 64
LONGEST = 4096


def seq_gather(rows, seq_count):
    spread = jnp.broadcast_to(rows[None], (seq_count,) + rows.shape)
    got = lax.all_to_all(spread, "seq", split_axis=0, concat_axis=0, tiled=True)
    return got.reshape((seq_count * rows.shape[0],) + rows.shape[1:])


def hid_scatter_sum(part):
    rows, width = part.shape
    z_count, y_count = lax.axis_size("zh"), lax.axis_size("y")
    cols = part.reshape(rows, z_count, y_count, width // (z_count * y_count))
    got = lax.all_to_all(cols, "y", split_axis=2, concat_axis=2, tiled=True)
    half = jnp.sum(got.astype(jnp.float32), axis=2)
    got = lax.all_to_all(half, "zh", split_axis=1, concat_axis=1, tiled=True)
    return jnp.sum(got, axis=1)


def hid_gather(cols):
    rows, col_count = cols.shape
    z_count, y_count = lax.axis_size("zh"), lax.axis_size("y")
    spread = jnp.broadcast_to(cols[:, None, :], (rows, z_count, col_count))
    got = lax.all_to_all(spread, "zh", split_axis=1, concat_axis=1, tiled=True)
    spread = jnp.broadcast_to(got[:, :, None, :], (rows, z_count, y_count, col_count))
    got = lax.all_to_all(spread, "y", split_axis=2, concat_axis=2, tiled=True)
    return got.reshape(rows, z_count * y_count * col_count)


def route_ranks(flat_ids):
    span = 64
    blocks = flat_ids.shape[0] // span
    onehot = (flat_ids[:, None] == jnp.arange(EXPERTS, dtype=jnp.int32)[None, :]).astype(
        jnp.bfloat16
    )
    onehot = onehot.reshape(blocks, span, EXPERTS)
    lower = jnp.arange(span)[:, None] >= jnp.arange(span)[None, :]
    within = jnp.einsum(
        "ij,bjk->bik", lower.astype(jnp.bfloat16), onehot, preferred_element_type=jnp.float32
    )
    earlier = jnp.arange(blocks)[:, None] > jnp.arange(blocks)[None, :]
    before = jnp.dot(
        earlier.astype(jnp.bfloat16),
        within[:, -1, :].astype(jnp.bfloat16),
        preferred_element_type=jnp.float32,
    )
    counts = within + before[:, None, :]
    ranks = jnp.sum(counts * onehot.astype(jnp.float32), axis=2) - 1.0
    return ranks.astype(jnp.int32).reshape(-1)


def on_device(
    stream,
    queries,
    key_rows,
    value_rows,
    segment_ids,
    out_proj,
    norm_gain,
    expert_ids,
    route_gates,
    gate_proj,
    up_proj,
    down_proj,
    shared_gate,
    shared_up,
    shared_down,
):
    tok_count = queries.shape[0]
    local_heads = queries.shape[1]
    head_width = queries.shape[2]
    width = stream.shape[1]
    inv_root = head_width ** (-0.5)
    seq_count = lax.axis_size("seq")
    hid_count = lax.axis_size("zh") * lax.axis_size("y")
    hid_index = lax.axis_index("zh") * lax.axis_size("y") + lax.axis_index("y")
    query_first = lax.axis_index("seq") * tok_count
    query_seg = lax.dynamic_slice_in_dim(segment_ids, query_first, tok_count)
    query_pos = query_first + jnp.arange(tok_count, dtype=jnp.int32)
    run_max = jnp.full((tok_count, local_heads), -1e30, jnp.float32)
    window = min(seq_count, -(-LONGEST // tok_count) + 1)
    both = jnp.concatenate([key_rows, value_rows], axis=1)
    blocks = [both]
    for shift in range(1, window):
        pairs = [(i, i + shift) for i in range(seq_count - shift)]
        blocks.append(lax.ppermute(both, "seq", pairs))
    both_win = jnp.concatenate(blocks[::-1], axis=0)
    key_part = both_win[:, :local_heads]
    value_part = both_win[:, local_heads:]
    row_count = key_part.shape[0]
    key_first = query_first - (window - 1) * tok_count
    key_pos = key_first + jnp.arange(row_count, dtype=jnp.int32)
    seg_padded = jnp.concatenate(
        [jnp.full(((window - 1) * tok_count,), -1, jnp.int32), segment_ids]
    )
    key_seg = lax.dynamic_slice_in_dim(seg_padded, query_first, row_count)
    scores = (
        jnp.einsum("qhd,khd->qhk", queries, key_part, preferred_element_type=jnp.float32) * inv_root
    )
    allowed = (query_seg[:, None] == key_seg[None, :]) & (
        key_pos[None, :] <= query_pos[:, None]
    )
    scores = jnp.where(allowed[:, None, :], scores, -1e30)
    new_max = jnp.maximum(run_max, jnp.max(scores, axis=2))
    weights = jnp.where(allowed[:, None, :], jnp.exp(scores - new_max[:, :, None]), 0.0)
    new_sum = jnp.sum(weights, axis=2)
    probs = weights.astype(jnp.bfloat16)
    new_acc = jnp.einsum("qhk,khd->qhd", probs, value_part, preferred_element_type=jnp.float32)
    attended = (
        (new_acc / new_sum[:, :, None])
        .astype(jnp.bfloat16)
        .reshape(tok_count, local_heads * head_width)
    )
    out_flat = out_proj.reshape(local_heads * head_width, width)
    partial_mix = jnp.dot(attended, out_flat, preferred_element_type=jnp.float32)
    col_count = width // hid_count
    col_first = hid_index * col_count
    mixed_cols = lax.dynamic_slice_in_dim(stream, col_first, col_count, 1).astype(
        jnp.float32
    ) + hid_scatter_sum(partial_mix.astype(jnp.bfloat16))
    mixed_all = hid_gather(mixed_cols.astype(jnp.bfloat16)).astype(jnp.float32)
    mean_square = jnp.mean(mixed_all * mixed_all, axis=1, keepdims=True)
    normed = (mixed_all * lax.rsqrt(mean_square + 1e-06) * norm_gain).astype(jnp.bfloat16)
    shared_gate_val = jnp.einsum(
        "td,fd->tf", normed, shared_gate, preferred_element_type=jnp.float32
    )
    shared_up_val = jnp.einsum("td,fd->tf", normed, shared_up, preferred_element_type=jnp.float32)
    shared_act = (jax.nn.silu(shared_gate_val) * shared_up_val).astype(jnp.bfloat16)
    shared_part = jnp.dot(shared_act, shared_down, preferred_element_type=jnp.float32)
    shared_out = hid_scatter_sum(shared_part.astype(jnp.bfloat16))
    unit_rows = gate_proj.shape[0]
    held_count = max(1, unit_rows // FF)
    held_units = unit_rows // held_count
    local_experts = EXPERTS // seq_count
    first_local = hid_index * unit_rows // FF
    flat_ids = expert_ids.reshape(-1)
    slot_rank = route_ranks(flat_ids)
    owner_group = flat_ids // local_experts
    local_expert = flat_ids % local_experts
    held_offset = local_expert - first_local
    is_held = (held_offset >= 0) & (held_offset < held_count)
    slot_total = seq_count * held_count * CAP
    send_index = jnp.where(
        is_held, (owner_group * held_count + held_offset) * CAP + slot_rank, slot_total
    )
    slot_ids = jnp.arange(slot_total, dtype=jnp.int32)
    picks = jnp.any(
        send_index.reshape(tok_count, TOP)[None, :, :] == slot_ids[:, None, None], axis=2
    ).astype(jnp.bfloat16)
    send_rows = jnp.dot(picks, normed, preferred_element_type=jnp.float32).astype(jnp.bfloat16)
    send_rows = send_rows.reshape(seq_count, held_count, CAP, width)
    received = lax.all_to_all(send_rows, "seq", split_axis=0, concat_axis=0, tiled=True)
    gate_local = gate_proj.reshape(held_count, held_units, width)
    up_local = up_proj.reshape(held_count, held_units, width)
    down_local = down_proj.reshape(held_count, held_units, width)
    gate_val = jnp.einsum(
        "sicd,ifd->sicf", received, gate_local, preferred_element_type=jnp.float32
    )
    up_val = jnp.einsum("sicd,ifd->sicf", received, up_local, preferred_element_type=jnp.float32)
    expert_act = (jax.nn.silu(gate_val) * up_val).astype(jnp.bfloat16)
    down_part = jnp.einsum(
        "sicf,ifd->iscd", expert_act, down_local, preferred_element_type=jnp.float32
    ).astype(jnp.bfloat16)
    z_count, y_count = lax.axis_size("zh"), lax.axis_size("y")
    down_part = down_part.reshape(seq_count * CAP, z_count, y_count, col_count)
    got = lax.all_to_all(down_part, "y", split_axis=2, concat_axis=2, tiled=True)
    summed = jnp.sum(got.astype(jnp.float32), axis=2).astype(jnp.bfloat16)
    got = lax.all_to_all(summed, "zh", split_axis=1, concat_axis=1, tiled=True)
    expert_out = got.transpose(1, 0, 2)
    returned = lax.all_to_all(
        expert_out.reshape(local_experts, seq_count, CAP, col_count),
        "seq",
        split_axis=1,
        concat_axis=1,
        tiled=True,
    ).reshape(-1, col_count)
    pick_index = local_expert * (seq_count * CAP) + owner_group * CAP + slot_rank
    picked = returned[pick_index].reshape(tok_count, TOP, col_count)
    routed_sum = jnp.einsum("tj,tjd->td", route_gates, picked.astype(jnp.float32))
    return (mixed_cols + shared_out + routed_sum).astype(jnp.bfloat16)


def solution(mesh):
    y_count = 4
    split_mesh = Mesh(
        mesh.devices.reshape(mesh.shape["seq"], mesh.shape["hid"] // y_count, y_count),
        ("seq", "zh", "y"),
    )
    hid = ("zh", "y")
    placed = (
        P("seq", None),
        P("seq", hid, None),
        P("seq", hid, None),
        P("seq", hid, None),
        P(),
        P(hid, None, None),
        P(),
        P("seq", None),
        P("seq", None),
        P(("seq",) + hid, None),
        P(("seq",) + hid, None),
        P(("seq",) + hid, None),
        P(hid, None),
        P(hid, None),
        P(hid, None),
    )
    return jax.shard_map(
        on_device, mesh=split_mesh, in_specs=placed, out_specs=P("seq", hid), check_vma=False
    )
```

```python
import jax
import jax.numpy as jnp
from jax import lax
from jax.sharding import Mesh, PartitionSpec as P

EXPERTS = 64
FF = 1408
TOP = 6
CAP = 64
LONGEST = 4096


def seq_gather(rows, seq_count):
    spread = jnp.broadcast_to(rows[None], (seq_count,) + rows.shape)
    got = lax.all_to_all(spread, "seq", split_axis=0, concat_axis=0, tiled=True)
    return got.reshape((seq_count * rows.shape[0],) + rows.shape[1:])


def hid_scatter_sum(part):
    got = lax.all_to_all(part, "y", split_axis=1, concat_axis=1, tiled=True)
    half = jnp.sum(got.astype(jnp.float32), axis=1).astype(jnp.bfloat16)
    got = lax.all_to_all(half, "zh", split_axis=0, concat_axis=0, tiled=True)
    return jnp.sum(got.astype(jnp.float32), axis=0)


def hid_reduce_pair(routed, shared):
    routed_rows = routed.shape[2]
    both = jnp.concatenate([routed, shared], axis=2)
    got = lax.all_to_all(both, "y", split_axis=1, concat_axis=1, tiled=True)
    half = jnp.sum(got.astype(jnp.float32), axis=1).astype(jnp.bfloat16)
    got = lax.all_to_all(half, "zh", split_axis=0, concat_axis=0, tiled=True)
    shared_sum = jnp.sum(got[:, routed_rows:].astype(jnp.float32), axis=0)
    return got[:, :routed_rows], shared_sum


def hid_gather(cols):
    rows, col_count = cols.shape
    z_count, y_count = lax.axis_size("zh"), lax.axis_size("y")
    spread = jnp.broadcast_to(cols[:, None, :], (rows, z_count, col_count))
    got = lax.all_to_all(spread, "zh", split_axis=1, concat_axis=1, tiled=True)
    spread = jnp.broadcast_to(got[:, :, None, :], (rows, z_count, y_count, col_count))
    got = lax.all_to_all(spread, "y", split_axis=2, concat_axis=2, tiled=True)
    return got.reshape(rows, z_count * y_count * col_count)


def route_ranks(flat_ids):
    span = 64
    blocks = flat_ids.shape[0] // span
    onehot = (flat_ids[:, None] == jnp.arange(EXPERTS, dtype=jnp.int32)[None, :]).astype(
        jnp.bfloat16
    )
    onehot = onehot.reshape(blocks, span, EXPERTS)
    lower = jnp.arange(span)[:, None] >= jnp.arange(span)[None, :]
    within = jnp.einsum(
        "ij,bjk->bik", lower.astype(jnp.bfloat16), onehot, preferred_element_type=jnp.float32
    )
    earlier = jnp.arange(blocks)[:, None] > jnp.arange(blocks)[None, :]
    before = jnp.dot(
        earlier.astype(jnp.bfloat16),
        within[:, -1, :].astype(jnp.bfloat16),
        preferred_element_type=jnp.float32,
    )
    counts = within + before[:, None, :]
    ranks = jnp.sum(counts * onehot.astype(jnp.float32), axis=2) - 1.0
    return ranks.astype(jnp.int32).reshape(-1)


def on_device(
    stream,
    queries,
    key_rows,
    value_rows,
    segment_ids,
    out_proj,
    norm_gain,
    expert_ids,
    route_gates,
    gate_proj,
    up_proj,
    down_proj,
    shared_gate,
    shared_up,
    shared_down,
):
    tok_count = queries.shape[0]
    local_heads = queries.shape[1]
    head_width = queries.shape[2]
    width = stream.shape[1]
    inv_root = head_width ** (-0.5)
    seq_count = lax.axis_size("seq")
    hid_count = lax.axis_size("zh") * lax.axis_size("y")
    hid_index = lax.axis_index("zh") * lax.axis_size("y") + lax.axis_index("y")
    query_first = lax.axis_index("seq") * tok_count
    query_seg = lax.dynamic_slice_in_dim(segment_ids, query_first, tok_count)
    query_pos = query_first + jnp.arange(tok_count, dtype=jnp.int32)
    run_max = jnp.full((tok_count, local_heads), -1e30, jnp.float32)
    window = min(seq_count, -(-LONGEST // tok_count) + 1)
    both = jnp.concatenate([key_rows, value_rows], axis=1)
    blocks = [both]
    for shift in range(1, window):
        pairs = [(i, i + shift) for i in range(seq_count - shift)]
        blocks.append(lax.ppermute(both, "seq", pairs))
    both_win = jnp.concatenate(blocks[::-1], axis=0)
    key_part = both_win[:, :local_heads]
    value_part = both_win[:, local_heads:]
    row_count = key_part.shape[0]
    key_first = query_first - (window - 1) * tok_count
    key_pos = key_first + jnp.arange(row_count, dtype=jnp.int32)
    seg_padded = jnp.concatenate(
        [jnp.full(((window - 1) * tok_count,), -1, jnp.int32), segment_ids]
    )
    key_seg = lax.dynamic_slice_in_dim(seg_padded, query_first, row_count)
    scores = (
        jnp.einsum("qhd,khd->qhk", queries, key_part, preferred_element_type=jnp.float32) * inv_root
    )
    allowed = (query_seg[:, None] == key_seg[None, :]) & (
        key_pos[None, :] <= query_pos[:, None]
    )
    scores = jnp.where(allowed[:, None, :], scores, -1e30)
    new_max = jnp.maximum(run_max, jnp.max(scores, axis=2))
    weights = jnp.where(allowed[:, None, :], jnp.exp(scores - new_max[:, :, None]), 0.0)
    new_sum = jnp.sum(weights, axis=2)
    probs = weights.astype(jnp.bfloat16)
    new_acc = jnp.einsum("qhk,khd->qhd", probs, value_part, preferred_element_type=jnp.float32)
    attended = (
        (new_acc / new_sum[:, :, None])
        .astype(jnp.bfloat16)
        .reshape(tok_count, local_heads * head_width)
    )
    z_count, y_count = lax.axis_size("zh"), lax.axis_size("y")
    out_flat = out_proj.reshape(local_heads * head_width, z_count, y_count, -1)
    partial_mix = jnp.einsum(
        "tk,kzyc->zytc", attended, out_flat, preferred_element_type=jnp.float32
    )
    col_count = width // hid_count
    col_first = hid_index * col_count
    mixed_cols = lax.dynamic_slice_in_dim(stream, col_first, col_count, 1).astype(
        jnp.float32
    ) + hid_scatter_sum(partial_mix.astype(jnp.bfloat16))
    mixed_all = hid_gather(mixed_cols.astype(jnp.bfloat16)).astype(jnp.float32)
    mean_square = jnp.mean(mixed_all * mixed_all, axis=1, keepdims=True)
    normed = (mixed_all * lax.rsqrt(mean_square + 1e-06) * norm_gain).astype(jnp.bfloat16)
    shared_gate_val = jnp.einsum(
        "td,fd->tf", normed, shared_gate, preferred_element_type=jnp.float32
    )
    shared_up_val = jnp.einsum("td,fd->tf", normed, shared_up, preferred_element_type=jnp.float32)
    shared_act = (jax.nn.silu(shared_gate_val) * shared_up_val).astype(jnp.bfloat16)
    shared_part = jnp.einsum(
        "tf,fzyc->zytc",
        shared_act,
        shared_down.reshape(shared_down.shape[0], z_count, y_count, col_count),
        preferred_element_type=jnp.float32,
    ).astype(jnp.bfloat16)
    unit_rows = gate_proj.shape[0]
    held_count = max(1, unit_rows // FF)
    held_units = unit_rows // held_count
    local_experts = EXPERTS // seq_count
    first_local = hid_index * unit_rows // FF
    flat_ids = expert_ids.reshape(-1)
    slot_rank = route_ranks(flat_ids)
    owner_group = flat_ids // local_experts
    local_expert = flat_ids % local_experts
    held_offset = local_expert - first_local
    is_held = (held_offset >= 0) & (held_offset < held_count)
    slot_total = seq_count * held_count * CAP
    send_index = jnp.where(
        is_held, (owner_group * held_count + held_offset) * CAP + slot_rank, slot_total
    )
    slot_ids = jnp.arange(slot_total, dtype=jnp.int32)
    picks = jnp.any(
        send_index.reshape(tok_count, TOP)[None, :, :] == slot_ids[:, None, None], axis=2
    ).astype(jnp.bfloat16)
    send_rows = jnp.dot(picks, normed, preferred_element_type=jnp.float32).astype(jnp.bfloat16)
    send_rows = send_rows.reshape(seq_count, held_count, CAP, width)
    received = lax.all_to_all(send_rows, "seq", split_axis=0, concat_axis=0, tiled=True)
    gate_local = gate_proj.reshape(held_count, held_units, width)
    up_local = up_proj.reshape(held_count, held_units, width)
    down_local = down_proj.reshape(held_count, held_units, z_count, y_count, col_count)
    gate_val = jnp.einsum(
        "sicd,ifd->sicf", received, gate_local, preferred_element_type=jnp.float32
    )
    up_val = jnp.einsum("sicd,ifd->sicf", received, up_local, preferred_element_type=jnp.float32)
    expert_act = (jax.nn.silu(gate_val) * up_val).astype(jnp.bfloat16)
    down_part = jnp.einsum(
        "sicf,ifzyx->zyscx", expert_act, down_local, preferred_element_type=jnp.float32
    ).astype(jnp.bfloat16)
    down_part = down_part.reshape(z_count, y_count, seq_count * CAP, col_count)
    expert_out, shared_out = hid_reduce_pair(down_part, shared_part)
    returned = lax.all_to_all(
        expert_out.reshape(local_experts, seq_count, CAP, col_count),
        "seq",
        split_axis=1,
        concat_axis=1,
        tiled=True,
    ).reshape(-1, col_count)
    pick_index = local_expert * (seq_count * CAP) + owner_group * CAP + slot_rank
    picked = returned[pick_index].reshape(tok_count, TOP, col_count)
    routed_sum = jnp.einsum("tj,tjd->td", route_gates, picked.astype(jnp.float32))
    return (mixed_cols + shared_out + routed_sum).astype(jnp.bfloat16)


def solution(mesh):
    y_count = 4
    split_mesh = Mesh(
        mesh.devices.reshape(mesh.shape["seq"], mesh.shape["hid"] // y_count, y_count),
        ("seq", "zh", "y"),
    )
    hid = ("zh", "y")
    placed = (
        P("seq", None),
        P("seq", hid, None),
        P("seq", hid, None),
        P("seq", hid, None),
        P(),
        P(hid, None, None),
        P(),
        P("seq", None),
        P("seq", None),
        P(("seq",) + hid, None),
        P(("seq",) + hid, None),
        P(("seq",) + hid, None),
        P(hid, None),
        P(hid, None),
        P(hid, None),
    )
    return jax.shard_map(
        on_device, mesh=split_mesh, in_specs=placed, out_specs=P("seq", hid), check_vma=False
    )
```

```python
import jax
import jax.numpy as jnp
from jax import lax
from jax.sharding import Mesh, PartitionSpec as P

EXPERTS = 64
FF = 1408
TOP = 6
CAP = 64
LONGEST = 4096


def seq_gather(rows, seq_count):
    spread = jnp.broadcast_to(rows[None], (seq_count,) + rows.shape)
    got = lax.all_to_all(spread, "seq", split_axis=0, concat_axis=0, tiled=True)
    return got.reshape((seq_count * rows.shape[0],) + rows.shape[1:])


def hid_scatter_sum(part):
    got = lax.all_to_all(part, "y", split_axis=1, concat_axis=1, tiled=True)
    half = jnp.sum(got.astype(jnp.float32), axis=1).astype(jnp.bfloat16)
    got = lax.all_to_all(half, "zh", split_axis=0, concat_axis=0, tiled=True)
    return jnp.sum(got.astype(jnp.float32), axis=0)


def hid_reduce_pair(routed, shared):
    routed_rows = routed.shape[2]
    both = jnp.concatenate([routed, shared], axis=2)
    got = lax.all_to_all(both, "y", split_axis=1, concat_axis=1, tiled=True)
    half = jnp.sum(got.astype(jnp.float32), axis=1).astype(jnp.bfloat16)
    got = lax.all_to_all(half, "zh", split_axis=0, concat_axis=0, tiled=True)
    shared_sum = jnp.sum(got[:, routed_rows:].astype(jnp.float32), axis=0)
    return got[:, :routed_rows], shared_sum


def hid_gather(cols):
    rows, col_count = cols.shape
    z_count, y_count = lax.axis_size("zh"), lax.axis_size("y")
    spread = jnp.broadcast_to(cols[:, None, :], (rows, z_count, col_count))
    got = lax.all_to_all(spread, "zh", split_axis=1, concat_axis=1, tiled=True)
    spread = jnp.broadcast_to(got[:, :, None, :], (rows, z_count, y_count, col_count))
    got = lax.all_to_all(spread, "y", split_axis=2, concat_axis=2, tiled=True)
    return got.reshape(rows, z_count * y_count * col_count)


def route_ranks(flat_ids):
    span = 64
    blocks = flat_ids.shape[0] // span
    onehot = (flat_ids[:, None] == jnp.arange(EXPERTS, dtype=jnp.int32)[None, :]).astype(
        jnp.bfloat16
    )
    onehot = onehot.reshape(blocks, span, EXPERTS)
    lower = jnp.arange(span)[:, None] >= jnp.arange(span)[None, :]
    within = jnp.einsum(
        "ij,bjk->bik", lower.astype(jnp.bfloat16), onehot, preferred_element_type=jnp.float32
    )
    earlier = jnp.arange(blocks)[:, None] > jnp.arange(blocks)[None, :]
    before = jnp.dot(
        earlier.astype(jnp.bfloat16),
        within[:, -1, :].astype(jnp.bfloat16),
        preferred_element_type=jnp.float32,
    )
    counts = within + before[:, None, :]
    ranks = jnp.sum(counts * onehot.astype(jnp.float32), axis=2) - 1.0
    return ranks.astype(jnp.int32).reshape(-1)


def on_device(
    stream,
    queries,
    key_rows,
    value_rows,
    segment_ids,
    out_proj,
    norm_gain,
    expert_ids,
    route_gates,
    gate_proj,
    up_proj,
    down_proj,
    shared_gate,
    shared_up,
    shared_down,
):
    tok_count = queries.shape[0]
    local_heads = queries.shape[1]
    head_width = queries.shape[2]
    width = stream.shape[1]
    inv_root = head_width ** (-0.5)
    seq_count = lax.axis_size("seq")
    hid_count = lax.axis_size("zh") * lax.axis_size("y")
    hid_index = lax.axis_index("zh") * lax.axis_size("y") + lax.axis_index("y")
    query_first = lax.axis_index("seq") * tok_count
    query_seg = lax.dynamic_slice_in_dim(segment_ids, query_first, tok_count)
    query_pos = query_first + jnp.arange(tok_count, dtype=jnp.int32)
    run_max = jnp.full((tok_count, local_heads), -1e30, jnp.float32)
    window = min(seq_count, -(-LONGEST // tok_count) + 1)
    both = jnp.concatenate([key_rows, value_rows], axis=1)
    blocks = [both]
    for shift in range(1, window):
        pairs = [(i, i + shift) for i in range(seq_count - shift)]
        blocks.append(lax.ppermute(both, "seq", pairs))
    both_win = jnp.concatenate(blocks[::-1], axis=0)
    key_part = both_win[:, :local_heads]
    value_part = both_win[:, local_heads:]
    row_count = key_part.shape[0]
    key_first = query_first - (window - 1) * tok_count
    key_pos = key_first + jnp.arange(row_count, dtype=jnp.int32)
    seg_padded = jnp.concatenate(
        [jnp.full(((window - 1) * tok_count,), -1, jnp.int32), segment_ids]
    )
    key_seg = lax.dynamic_slice_in_dim(seg_padded, query_first, row_count)
    scores = (
        jnp.einsum("qhd,khd->qhk", queries, key_part, preferred_element_type=jnp.float32) * inv_root
    )
    allowed = (query_seg[:, None] == key_seg[None, :]) & (
        key_pos[None, :] <= query_pos[:, None]
    )
    scores = jnp.where(allowed[:, None, :], scores, -1e30)
    new_max = jnp.maximum(run_max, jnp.max(scores, axis=2))
    weights = jnp.where(allowed[:, None, :], jnp.exp(scores - new_max[:, :, None]), 0.0)
    new_sum = jnp.sum(weights, axis=2)
    probs = weights.astype(jnp.bfloat16)
    new_acc = jnp.einsum("qhk,khd->qhd", probs, value_part, preferred_element_type=jnp.float32)
    attended = (
        (new_acc / new_sum[:, :, None])
        .astype(jnp.bfloat16)
        .reshape(tok_count, local_heads * head_width)
    )
    z_count, y_count = lax.axis_size("zh"), lax.axis_size("y")
    out_flat = out_proj.reshape(local_heads * head_width, z_count * y_count, -1)
    partial_mix = jnp.einsum(
        "tk,kjc->jtc", attended, out_flat, preferred_element_type=jnp.float32
    ).reshape(z_count, y_count, tok_count, -1)
    col_count = width // hid_count
    col_first = hid_index * col_count
    mixed_cols = lax.dynamic_slice_in_dim(stream, col_first, col_count, 1).astype(
        jnp.float32
    ) + hid_scatter_sum(partial_mix.astype(jnp.bfloat16))
    mixed_all = hid_gather(mixed_cols.astype(jnp.bfloat16)).astype(jnp.float32)
    mean_square = jnp.mean(mixed_all * mixed_all, axis=1, keepdims=True)
    normed = (mixed_all * lax.rsqrt(mean_square + 1e-06) * norm_gain).astype(jnp.bfloat16)
    shared_gate_val = jnp.einsum(
        "td,fd->tf", normed, shared_gate, preferred_element_type=jnp.float32
    )
    shared_up_val = jnp.einsum("td,fd->tf", normed, shared_up, preferred_element_type=jnp.float32)
    shared_act = (jax.nn.silu(shared_gate_val) * shared_up_val).astype(jnp.bfloat16)
    shared_part = (
        jnp.einsum(
            "tf,fjc->jtc",
            shared_act,
            shared_down.reshape(shared_down.shape[0], hid_count, col_count),
            preferred_element_type=jnp.float32,
        )
        .astype(jnp.bfloat16)
        .reshape(z_count, y_count, tok_count, col_count)
    )
    unit_rows = gate_proj.shape[0]
    held_count = max(1, unit_rows // FF)
    held_units = unit_rows // held_count
    local_experts = EXPERTS // seq_count
    first_local = hid_index * unit_rows // FF
    flat_ids = expert_ids.reshape(-1)
    slot_rank = route_ranks(flat_ids)
    owner_group = flat_ids // local_experts
    local_expert = flat_ids % local_experts
    held_offset = local_expert - first_local
    is_held = (held_offset >= 0) & (held_offset < held_count)
    slot_total = seq_count * held_count * CAP
    send_index = jnp.where(
        is_held, (owner_group * held_count + held_offset) * CAP + slot_rank, slot_total
    )
    slot_ids = jnp.arange(slot_total, dtype=jnp.int32)
    picks = jnp.any(
        send_index.reshape(tok_count, TOP)[None, :, :] == slot_ids[:, None, None], axis=2
    ).astype(jnp.bfloat16)
    send_rows = jnp.dot(picks, normed, preferred_element_type=jnp.float32).astype(jnp.bfloat16)
    send_rows = send_rows.reshape(seq_count, held_count, CAP, width)
    received = lax.all_to_all(send_rows, "seq", split_axis=0, concat_axis=0, tiled=True)
    gate_local = gate_proj.reshape(held_count, held_units, width)
    up_local = up_proj.reshape(held_count, held_units, width)
    down_local = down_proj.reshape(held_count, held_units, hid_count, col_count)
    gate_val = jnp.einsum(
        "sicd,ifd->sicf", received, gate_local, preferred_element_type=jnp.float32
    )
    up_val = jnp.einsum("sicd,ifd->sicf", received, up_local, preferred_element_type=jnp.float32)
    expert_act = (jax.nn.silu(gate_val) * up_val).astype(jnp.bfloat16)
    down_part = jnp.einsum(
        "sicf,ifjx->jscx", expert_act, down_local, preferred_element_type=jnp.float32
    ).astype(jnp.bfloat16)
    down_part = down_part.reshape(z_count, y_count, seq_count * CAP, col_count)
    expert_out, shared_out = hid_reduce_pair(down_part, shared_part)
    returned = lax.all_to_all(
        expert_out.reshape(local_experts, seq_count, CAP, col_count),
        "seq",
        split_axis=1,
        concat_axis=1,
        tiled=True,
    ).reshape(-1, col_count)
    pick_index = local_expert * (seq_count * CAP) + owner_group * CAP + slot_rank
    picked = returned[pick_index].reshape(tok_count, TOP, col_count)
    routed_sum = jnp.einsum("tj,tjd->td", route_gates, picked.astype(jnp.float32))
    return (mixed_cols + shared_out + routed_sum).astype(jnp.bfloat16)


def solution(mesh):
    y_count = 4
    split_mesh = Mesh(
        mesh.devices.reshape(mesh.shape["seq"], mesh.shape["hid"] // y_count, y_count),
        ("seq", "zh", "y"),
    )
    hid = ("zh", "y")
    placed = (
        P("seq", None),
        P("seq", hid, None),
        P("seq", hid, None),
        P("seq", hid, None),
        P(),
        P(hid, None, None),
        P(),
        P("seq", None),
        P("seq", None),
        P(("seq",) + hid, None),
        P(("seq",) + hid, None),
        P(("seq",) + hid, None),
        P(hid, None),
        P(hid, None),
        P(hid, None),
    )
    return jax.shard_map(
        on_device, mesh=split_mesh, in_specs=placed, out_specs=P("seq", hid), check_vma=False
    )
```

```python
import jax
import jax.numpy as jnp
from jax import lax
from jax.sharding import Mesh, PartitionSpec as P

EXPERTS = 64
FF = 1408
TOP = 6
CAP = 64
LONGEST = 4096


def seq_gather(rows, seq_count):
    spread = jnp.broadcast_to(rows[None], (seq_count,) + rows.shape)
    got = lax.all_to_all(spread, "seq", split_axis=0, concat_axis=0, tiled=True)
    return got.reshape((seq_count * rows.shape[0],) + rows.shape[1:])


def hid_scatter_sum(part):
    got = lax.all_to_all(part, "y", split_axis=1, concat_axis=1, tiled=True)
    half = jnp.sum(got.astype(jnp.float32), axis=1).astype(jnp.bfloat16)
    got = lax.all_to_all(half, "zh", split_axis=0, concat_axis=0, tiled=True)
    return jnp.sum(got.astype(jnp.float32), axis=0)


def hid_reduce_pair(routed, shared):
    routed_rows = routed.shape[2]
    both = jnp.concatenate([routed, shared], axis=2)
    got = lax.all_to_all(both, "y", split_axis=1, concat_axis=1, tiled=True)
    half = jnp.sum(got.astype(jnp.float32), axis=1).astype(jnp.bfloat16)
    got = lax.all_to_all(half, "zh", split_axis=0, concat_axis=0, tiled=True)
    shared_sum = jnp.sum(got[:, routed_rows:].astype(jnp.float32), axis=0)
    return got[:, :routed_rows], shared_sum


def hid_gather(cols):
    rows, col_count = cols.shape
    z_count, y_count = lax.axis_size("zh"), lax.axis_size("y")
    spread = jnp.broadcast_to(cols[:, None, :], (rows, z_count, col_count))
    got = lax.all_to_all(spread, "zh", split_axis=1, concat_axis=1, tiled=True)
    spread = jnp.broadcast_to(got[:, :, None, :], (rows, z_count, y_count, col_count))
    got = lax.all_to_all(spread, "y", split_axis=2, concat_axis=2, tiled=True)
    return got.reshape(rows, z_count * y_count * col_count)


def route_ranks(flat_ids):
    span = 64
    blocks = flat_ids.shape[0] // span
    onehot = (flat_ids[:, None] == jnp.arange(EXPERTS, dtype=jnp.int32)[None, :]).astype(
        jnp.bfloat16
    )
    onehot = onehot.reshape(blocks, span, EXPERTS)
    lower = jnp.arange(span)[:, None] >= jnp.arange(span)[None, :]
    within = jnp.einsum(
        "ij,bjk->bik", lower.astype(jnp.bfloat16), onehot, preferred_element_type=jnp.float32
    )
    earlier = jnp.arange(blocks)[:, None] > jnp.arange(blocks)[None, :]
    before = jnp.dot(
        earlier.astype(jnp.bfloat16),
        within[:, -1, :].astype(jnp.bfloat16),
        preferred_element_type=jnp.float32,
    )
    counts = within + before[:, None, :]
    ranks = jnp.sum(counts * onehot.astype(jnp.float32), axis=2) - 1.0
    return ranks.astype(jnp.int32).reshape(-1)


def on_device(
    stream,
    queries,
    key_rows,
    value_rows,
    segment_ids,
    out_proj,
    norm_gain,
    expert_ids,
    route_gates,
    gate_proj,
    up_proj,
    down_proj,
    shared_gate,
    shared_up,
    shared_down,
):
    tok_count = queries.shape[0]
    local_heads = queries.shape[1]
    head_width = queries.shape[2]
    width = stream.shape[1]
    inv_root = head_width ** (-0.5)
    seq_count = lax.axis_size("seq")
    hid_count = lax.axis_size("zh") * lax.axis_size("y")
    hid_index = lax.axis_index("zh") * lax.axis_size("y") + lax.axis_index("y")
    query_first = lax.axis_index("seq") * tok_count
    query_seg = lax.dynamic_slice_in_dim(segment_ids, query_first, tok_count)
    query_pos = query_first + jnp.arange(tok_count, dtype=jnp.int32)
    run_max = jnp.full((tok_count, local_heads), -1e30, jnp.float32)
    window = min(seq_count, -(-LONGEST // tok_count) + 1)
    both = jnp.concatenate([key_rows, value_rows], axis=1)
    blocks = [both]
    for shift in range(1, window):
        pairs = [(i, i + shift) for i in range(seq_count - shift)]
        blocks.append(lax.ppermute(both, "seq", pairs))
    both_win = jnp.concatenate(blocks[::-1], axis=0)
    key_part = both_win[:, :local_heads]
    value_part = both_win[:, local_heads:]
    row_count = key_part.shape[0]
    key_first = query_first - (window - 1) * tok_count
    key_pos = key_first + jnp.arange(row_count, dtype=jnp.int32)
    seg_padded = jnp.concatenate(
        [jnp.full(((window - 1) * tok_count,), -1, jnp.int32), segment_ids]
    )
    key_seg = lax.dynamic_slice_in_dim(seg_padded, query_first, row_count)
    scores = (
        jnp.einsum("qhd,khd->qhk", queries, key_part, preferred_element_type=jnp.float32) * inv_root
    )
    allowed = (query_seg[:, None] == key_seg[None, :]) & (
        key_pos[None, :] <= query_pos[:, None]
    )
    scores = jnp.where(allowed[:, None, :], scores, -1e30)
    new_max = jnp.maximum(run_max, jnp.max(scores, axis=2))
    weights = jnp.where(allowed[:, None, :], jnp.exp(scores - new_max[:, :, None]), 0.0)
    new_sum = jnp.sum(weights, axis=2)
    probs = weights.astype(jnp.bfloat16)
    new_acc = jnp.einsum("qhk,khd->qhd", probs, value_part, preferred_element_type=jnp.float32)
    attended = (
        (new_acc / new_sum[:, :, None])
        .astype(jnp.bfloat16)
        .reshape(tok_count, local_heads * head_width)
    )
    z_count, y_count = lax.axis_size("zh"), lax.axis_size("y")
    out_flat = out_proj.reshape(local_heads * head_width, z_count, y_count, -1)
    partial_mix = jnp.einsum(
        "tk,kzyc->zytc", attended, out_flat, preferred_element_type=jnp.float32
    )
    col_count = width // hid_count
    col_first = hid_index * col_count
    mixed_cols = lax.dynamic_slice_in_dim(stream, col_first, col_count, 1).astype(
        jnp.float32
    ) + hid_scatter_sum(partial_mix.astype(jnp.bfloat16))
    mixed_all = hid_gather(mixed_cols.astype(jnp.bfloat16)).astype(jnp.float32)
    mean_square = jnp.mean(mixed_all * mixed_all, axis=1, keepdims=True)
    normed = (mixed_all * lax.rsqrt(mean_square + 1e-06) * norm_gain).astype(jnp.bfloat16)
    shared_gate_val = jnp.einsum(
        "td,fd->tf", normed, shared_gate, preferred_element_type=jnp.float32
    )
    shared_up_val = jnp.einsum("td,fd->tf", normed, shared_up, preferred_element_type=jnp.float32)
    shared_act = (jax.nn.silu(shared_gate_val) * shared_up_val).astype(jnp.bfloat16)
    shared_part = jnp.einsum(
        "tf,fzyc->zytc",
        shared_act,
        shared_down.reshape(shared_down.shape[0], z_count, y_count, col_count),
        preferred_element_type=jnp.float32,
    ).astype(jnp.bfloat16)
    unit_rows = gate_proj.shape[0]
    held_count = max(1, unit_rows // FF)
    held_units = unit_rows // held_count
    local_experts = EXPERTS // seq_count
    first_local = hid_index * unit_rows // FF
    flat_ids = expert_ids.reshape(-1)
    slot_rank = route_ranks(flat_ids)
    owner_group = flat_ids // local_experts
    local_expert = flat_ids % local_experts
    held_offset = local_expert - first_local
    is_held = (held_offset >= 0) & (held_offset < held_count)
    slot_total = seq_count * held_count * CAP
    send_index = jnp.where(
        is_held, (owner_group * held_count + held_offset) * CAP + slot_rank, slot_total
    )
    slot_ids = jnp.arange(slot_total, dtype=jnp.int32)
    picks = jnp.any(
        send_index.reshape(tok_count, TOP)[None, :, :] == slot_ids[:, None, None], axis=2
    ).astype(jnp.bfloat16)
    send_rows = jnp.dot(picks, normed, preferred_element_type=jnp.float32).astype(jnp.bfloat16)
    send_rows = send_rows.reshape(seq_count, held_count, CAP, width)
    received = lax.all_to_all(send_rows, "seq", split_axis=0, concat_axis=0, tiled=True)
    gate_local = gate_proj.reshape(held_count, held_units, width)
    up_local = up_proj.reshape(held_count, held_units, width)
    down_local = down_proj.reshape(held_count, held_units, z_count, y_count, col_count)
    gate_val = jnp.einsum(
        "sicd,ifd->sicf", received, gate_local, preferred_element_type=jnp.float32
    )
    up_val = jnp.einsum("sicd,ifd->sicf", received, up_local, preferred_element_type=jnp.float32)
    expert_act = (jax.nn.silu(gate_val) * up_val).astype(jnp.bfloat16)
    down_part = jnp.einsum(
        "sicf,ifzyx->zyscx", expert_act, down_local, preferred_element_type=jnp.float32
    ).astype(jnp.bfloat16)
    down_part = down_part.reshape(z_count, y_count, seq_count * CAP, col_count)
    expert_out, shared_out = hid_reduce_pair(down_part, shared_part)
    returned = lax.all_to_all(
        expert_out.reshape(local_experts, seq_count, CAP, col_count),
        "seq",
        split_axis=1,
        concat_axis=1,
        tiled=True,
    ).reshape(-1, col_count)
    pick_index = local_expert * (seq_count * CAP) + owner_group * CAP + slot_rank
    row_ids = jnp.arange(returned.shape[0], dtype=jnp.int32)
    hits = pick_index.reshape(tok_count, TOP)[:, :, None] == row_ids[None, None, :]
    weights = jnp.sum(jnp.where(hits, route_gates[:, :, None], 0.0), axis=1)
    weights_hi = weights.astype(jnp.bfloat16)
    weights_lo = (weights - weights_hi.astype(jnp.float32)).astype(jnp.bfloat16)
    routed_sum = jnp.dot(weights_hi, returned, preferred_element_type=jnp.float32) + jnp.dot(
        weights_lo, returned, preferred_element_type=jnp.float32
    )
    return (mixed_cols + shared_out + routed_sum).astype(jnp.bfloat16)


def solution(mesh):
    y_count = 4
    split_mesh = Mesh(
        mesh.devices.reshape(mesh.shape["seq"], mesh.shape["hid"] // y_count, y_count),
        ("seq", "zh", "y"),
    )
    hid = ("zh", "y")
    placed = (
        P("seq", None),
        P("seq", hid, None),
        P("seq", hid, None),
        P("seq", hid, None),
        P(),
        P(hid, None, None),
        P(),
        P("seq", None),
        P("seq", None),
        P(("seq",) + hid, None),
        P(("seq",) + hid, None),
        P(("seq",) + hid, None),
        P(hid, None),
        P(hid, None),
        P(hid, None),
    )
    return jax.shard_map(
        on_device, mesh=split_mesh, in_specs=placed, out_specs=P("seq", hid), check_vma=False
    )
```

```python
import jax
import jax.numpy as jnp
from jax import lax
from jax.sharding import Mesh, PartitionSpec as P

EXPERTS = 64
FF = 1408
TOP = 6
CAP = 64
LONGEST = 4096


def seq_gather(rows, seq_count):
    spread = jnp.broadcast_to(rows[None], (seq_count,) + rows.shape)
    got = lax.all_to_all(spread, "seq", split_axis=0, concat_axis=0, tiled=True)
    return got.reshape((seq_count * rows.shape[0],) + rows.shape[1:])


def hid_scatter_sum(part):
    got = lax.all_to_all(part, "y", split_axis=1, concat_axis=1, tiled=True)
    half = jnp.sum(got.astype(jnp.float32), axis=1).astype(jnp.bfloat16)
    got = lax.all_to_all(half, "zh", split_axis=0, concat_axis=0, tiled=True)
    return jnp.sum(got.astype(jnp.float32), axis=0)


def hid_reduce_pair(routed, shared):
    routed_rows = routed.shape[2]
    both = jnp.concatenate([routed, shared], axis=2)
    got = lax.all_to_all(both, "y", split_axis=1, concat_axis=1, tiled=True)
    half = jnp.sum(got.astype(jnp.float32), axis=1).astype(jnp.bfloat16)
    got = lax.all_to_all(half, "zh", split_axis=0, concat_axis=0, tiled=True)
    shared_sum = jnp.sum(got[:, routed_rows:].astype(jnp.float32), axis=0)
    return got[:, :routed_rows], shared_sum


def hid_gather(cols):
    rows, col_count = cols.shape
    z_count, y_count = lax.axis_size("zh"), lax.axis_size("y")
    spread = jnp.broadcast_to(cols[:, None, :], (rows, z_count, col_count))
    got = lax.all_to_all(spread, "zh", split_axis=1, concat_axis=1, tiled=True)
    spread = jnp.broadcast_to(got[:, :, None, :], (rows, z_count, y_count, col_count))
    got = lax.all_to_all(spread, "y", split_axis=2, concat_axis=2, tiled=True)
    return got.reshape(rows, z_count * y_count * col_count)


def route_ranks(flat_ids):
    span = 64
    blocks = flat_ids.shape[0] // span
    onehot = (flat_ids[:, None] == jnp.arange(EXPERTS, dtype=jnp.int32)[None, :]).astype(
        jnp.bfloat16
    )
    onehot = onehot.reshape(blocks, span, EXPERTS)
    lower = jnp.arange(span)[:, None] >= jnp.arange(span)[None, :]
    within = jnp.einsum(
        "ij,bjk->bik", lower.astype(jnp.bfloat16), onehot, preferred_element_type=jnp.float32
    )
    earlier = jnp.arange(blocks)[:, None] > jnp.arange(blocks)[None, :]
    before = jnp.dot(
        earlier.astype(jnp.bfloat16),
        within[:, -1, :].astype(jnp.bfloat16),
        preferred_element_type=jnp.float32,
    )
    counts = within + before[:, None, :]
    ranks = jnp.sum(counts * onehot.astype(jnp.float32), axis=2) - 1.0
    return ranks.astype(jnp.int32).reshape(-1)


def on_device(
    stream,
    queries,
    key_rows,
    value_rows,
    segment_ids,
    out_proj,
    norm_gain,
    expert_ids,
    route_gates,
    gate_proj,
    up_proj,
    down_proj,
    shared_gate,
    shared_up,
    shared_down,
):
    tok_count = queries.shape[0]
    local_heads = queries.shape[1]
    head_width = queries.shape[2]
    width = stream.shape[1]
    inv_root = head_width ** (-0.5)
    seq_count = lax.axis_size("seq")
    hid_count = lax.axis_size("zh") * lax.axis_size("y")
    hid_index = lax.axis_index("zh") * lax.axis_size("y") + lax.axis_index("y")
    query_first = lax.axis_index("seq") * tok_count
    query_seg = lax.dynamic_slice_in_dim(segment_ids, query_first, tok_count)
    query_pos = query_first + jnp.arange(tok_count, dtype=jnp.int32)
    run_max = jnp.full((tok_count, local_heads), -1e30, jnp.float32)
    window = min(seq_count, -(-LONGEST // tok_count) + 1)
    both = jnp.concatenate([key_rows, value_rows], axis=1)
    blocks = [both]
    for shift in range(1, window):
        pairs = [(i, i + shift) for i in range(seq_count - shift)]
        blocks.append(lax.ppermute(both, "seq", pairs))
    both_win = jnp.concatenate(blocks[::-1], axis=0)
    key_part = both_win[:, :local_heads]
    value_part = both_win[:, local_heads:]
    row_count = key_part.shape[0]
    key_first = query_first - (window - 1) * tok_count
    key_pos = key_first + jnp.arange(row_count, dtype=jnp.int32)
    seg_padded = jnp.concatenate(
        [jnp.full(((window - 1) * tok_count,), -1, jnp.int32), segment_ids]
    )
    key_seg = lax.dynamic_slice_in_dim(seg_padded, query_first, row_count)
    scores = (
        jnp.einsum("qhd,khd->qhk", queries, key_part, preferred_element_type=jnp.float32) * inv_root
    )
    allowed = (query_seg[:, None] == key_seg[None, :]) & (
        key_pos[None, :] <= query_pos[:, None]
    )
    scores = jnp.where(allowed[:, None, :], scores, -1e30)
    new_max = jnp.maximum(run_max, jnp.max(scores, axis=2))
    weights = jnp.where(allowed[:, None, :], jnp.exp(scores - new_max[:, :, None]), 0.0)
    new_sum = jnp.sum(weights, axis=2)
    probs = weights.astype(jnp.bfloat16)
    new_acc = jnp.einsum("qhk,khd->qhd", probs, value_part, preferred_element_type=jnp.float32)
    attended = (
        (new_acc / new_sum[:, :, None])
        .astype(jnp.bfloat16)
        .reshape(tok_count, local_heads * head_width)
    )
    z_count, y_count = lax.axis_size("zh"), lax.axis_size("y")
    out_flat = out_proj.reshape(local_heads * head_width, z_count, y_count, -1)
    partial_mix = jnp.einsum(
        "tk,kzyc->zytc", attended, out_flat, preferred_element_type=jnp.float32
    )
    col_count = width // hid_count
    col_first = hid_index * col_count
    mixed_cols = lax.dynamic_slice_in_dim(stream, col_first, col_count, 1).astype(
        jnp.float32
    ) + hid_scatter_sum(partial_mix.astype(jnp.bfloat16))
    mixed_all = hid_gather(mixed_cols.astype(jnp.bfloat16)).astype(jnp.float32)
    mean_square = jnp.mean(mixed_all * mixed_all, axis=1, keepdims=True)
    normed = (mixed_all * lax.rsqrt(mean_square + 1e-06) * norm_gain).astype(jnp.bfloat16)
    shared_gate_val = jnp.einsum(
        "td,fd->tf", normed, shared_gate, preferred_element_type=jnp.float32
    )
    shared_up_val = jnp.einsum("td,fd->tf", normed, shared_up, preferred_element_type=jnp.float32)
    shared_act = (jax.nn.silu(shared_gate_val) * shared_up_val).astype(jnp.bfloat16)
    shared_part = jnp.einsum(
        "tf,fzyc->zytc",
        shared_act,
        shared_down.reshape(shared_down.shape[0], z_count, y_count, col_count),
        preferred_element_type=jnp.float32,
    ).astype(jnp.bfloat16)
    unit_rows = gate_proj.shape[0]
    held_count = max(1, unit_rows // FF)
    held_units = unit_rows // held_count
    local_experts = EXPERTS // seq_count
    first_local = hid_index * unit_rows // FF
    flat_ids = expert_ids.reshape(-1)
    slot_rank = route_ranks(flat_ids)
    owner_group = flat_ids // local_experts
    local_expert = flat_ids % local_experts
    held_offset = local_expert - first_local
    is_held = (held_offset >= 0) & (held_offset < held_count)
    slot_total = seq_count * held_count * CAP
    send_index = jnp.where(
        is_held, (owner_group * held_count + held_offset) * CAP + slot_rank, slot_total
    )
    slot_ids = jnp.arange(slot_total, dtype=jnp.int32)
    picks = jnp.any(
        send_index.reshape(tok_count, TOP)[None, :, :] == slot_ids[:, None, None], axis=2
    ).astype(jnp.bfloat16)
    send_rows = jnp.dot(picks, normed, preferred_element_type=jnp.float32).astype(jnp.bfloat16)
    send_rows = send_rows.reshape(seq_count, held_count, CAP, width)
    received = lax.all_to_all(send_rows, "seq", split_axis=0, concat_axis=0, tiled=True)
    gate_local = gate_proj.reshape(held_count, held_units, width)
    up_local = up_proj.reshape(held_count, held_units, width)
    down_local = down_proj.reshape(held_count, held_units, z_count, y_count, col_count)
    gate_val = jnp.einsum(
        "sicd,ifd->sicf", received, gate_local, preferred_element_type=jnp.float32
    )
    up_val = jnp.einsum("sicd,ifd->sicf", received, up_local, preferred_element_type=jnp.float32)
    expert_act = (jax.nn.silu(gate_val) * up_val).astype(jnp.bfloat16)
    down_part = jnp.einsum(
        "sicf,ifzyx->zyscx", expert_act, down_local, preferred_element_type=jnp.float32
    ).astype(jnp.bfloat16)
    down_part = down_part.reshape(z_count, y_count, seq_count * CAP, col_count)
    expert_out, shared_out = hid_reduce_pair(down_part, shared_part)
    returned = lax.all_to_all(
        expert_out.reshape(local_experts, seq_count, CAP, col_count),
        "seq",
        split_axis=1,
        concat_axis=1,
        tiled=True,
    ).reshape(-1, col_count)
    pick_index = local_expert * (seq_count * CAP) + owner_group * CAP + slot_rank
    row_ids = jnp.arange(returned.shape[0], dtype=jnp.int32)
    hits = pick_index.reshape(tok_count, TOP)[:, :, None] == row_ids[None, None, :]
    gates_hi = route_gates.astype(jnp.bfloat16).astype(jnp.float32)
    gates_lo = route_gates - gates_hi
    weights_hi = jnp.sum(jnp.where(hits, gates_hi[:, :, None], 0.0), axis=1).astype(jnp.bfloat16)
    weights_lo = jnp.sum(jnp.where(hits, gates_lo[:, :, None], 0.0), axis=1).astype(jnp.bfloat16)
    routed_sum = jnp.dot(weights_hi, returned, preferred_element_type=jnp.float32) + jnp.dot(
        weights_lo, returned, preferred_element_type=jnp.float32
    )
    return (mixed_cols + shared_out + routed_sum).astype(jnp.bfloat16)


def solution(mesh):
    y_count = 4
    split_mesh = Mesh(
        mesh.devices.reshape(mesh.shape["seq"], mesh.shape["hid"] // y_count, y_count),
        ("seq", "zh", "y"),
    )
    hid = ("zh", "y")
    placed = (
        P("seq", None),
        P("seq", hid, None),
        P("seq", hid, None),
        P("seq", hid, None),
        P(),
        P(hid, None, None),
        P(),
        P("seq", None),
        P("seq", None),
        P(("seq",) + hid, None),
        P(("seq",) + hid, None),
        P(("seq",) + hid, None),
        P(hid, None),
        P(hid, None),
        P(hid, None),
    )
    return jax.shard_map(
        on_device, mesh=split_mesh, in_specs=placed, out_specs=P("seq", hid), check_vma=False
    )
```

```python
import jax
import jax.numpy as jnp
from jax import lax
from jax.sharding import Mesh, PartitionSpec as P

EXPERTS = 64
FF = 1408
TOP = 6
CAP = 64
LONGEST = 4096


def seq_gather(rows, seq_count):
    spread = jnp.broadcast_to(rows[None], (seq_count,) + rows.shape)
    got = lax.all_to_all(spread, "seq", split_axis=0, concat_axis=0, tiled=True)
    return got.reshape((seq_count * rows.shape[0],) + rows.shape[1:])


def hid_scatter_sum(part):
    got = lax.all_to_all(part, "y", split_axis=1, concat_axis=1, tiled=True)
    half = jnp.sum(got.astype(jnp.float32), axis=1).astype(jnp.bfloat16)
    got = lax.all_to_all(half, "zh", split_axis=0, concat_axis=0, tiled=True)
    return jnp.sum(got.astype(jnp.float32), axis=0)


def hid_reduce_pair(routed, shared):
    routed_rows = routed.shape[2]
    both = jnp.concatenate([routed, shared], axis=2)
    got = lax.all_to_all(both, "y", split_axis=1, concat_axis=1, tiled=True)
    half = jnp.sum(got.astype(jnp.float32), axis=1).astype(jnp.bfloat16)
    got = lax.all_to_all(half, "zh", split_axis=0, concat_axis=0, tiled=True)
    shared_sum = jnp.sum(got[:, routed_rows:].astype(jnp.float32), axis=0)
    return got[:, :routed_rows], shared_sum


def hid_gather(cols):
    rows, col_count = cols.shape
    z_count, y_count = lax.axis_size("zh"), lax.axis_size("y")
    spread = jnp.broadcast_to(cols[:, None, :], (rows, z_count, col_count))
    got = lax.all_to_all(spread, "zh", split_axis=1, concat_axis=1, tiled=True)
    spread = jnp.broadcast_to(got[:, :, None, :], (rows, z_count, y_count, col_count))
    got = lax.all_to_all(spread, "y", split_axis=2, concat_axis=2, tiled=True)
    return got.reshape(rows, z_count * y_count * col_count)


def route_ranks(flat_ids):
    span = 64
    blocks = flat_ids.shape[0] // span
    onehot = (flat_ids[:, None] == jnp.arange(EXPERTS, dtype=jnp.int32)[None, :]).astype(
        jnp.bfloat16
    )
    onehot = onehot.reshape(blocks, span, EXPERTS)
    lower = jnp.arange(span)[:, None] >= jnp.arange(span)[None, :]
    within = jnp.einsum(
        "ij,bjk->bik", lower.astype(jnp.bfloat16), onehot, preferred_element_type=jnp.float32
    )
    earlier = jnp.arange(blocks)[:, None] > jnp.arange(blocks)[None, :]
    before = jnp.dot(
        earlier.astype(jnp.bfloat16),
        within[:, -1, :].astype(jnp.bfloat16),
        preferred_element_type=jnp.float32,
    )
    counts = within + before[:, None, :]
    ranks = jnp.sum(counts * onehot.astype(jnp.float32), axis=2) - 1.0
    return ranks.astype(jnp.int32).reshape(-1)


def on_device(
    stream,
    queries,
    key_rows,
    value_rows,
    segment_ids,
    out_proj,
    norm_gain,
    expert_ids,
    route_gates,
    gate_proj,
    up_proj,
    down_proj,
    shared_gate,
    shared_up,
    shared_down,
):
    tok_count = queries.shape[0]
    local_heads = queries.shape[1]
    head_width = queries.shape[2]
    width = stream.shape[1]
    inv_root = head_width ** (-0.5)
    seq_count = lax.axis_size("seq")
    hid_count = lax.axis_size("zh") * lax.axis_size("y")
    hid_index = lax.axis_index("zh") * lax.axis_size("y") + lax.axis_index("y")
    query_first = lax.axis_index("seq") * tok_count
    query_seg = lax.dynamic_slice_in_dim(segment_ids, query_first, tok_count)
    query_pos = query_first + jnp.arange(tok_count, dtype=jnp.int32)
    run_max = jnp.full((tok_count, local_heads), -1e30, jnp.float32)
    window = min(seq_count, -(-LONGEST // tok_count) + 1)
    both = jnp.concatenate([key_rows, value_rows], axis=1)
    blocks = [both]
    for shift in range(1, window):
        pairs = [(i, i + shift) for i in range(seq_count - shift)]
        blocks.append(lax.ppermute(both, "seq", pairs))
    both_win = jnp.concatenate(blocks[::-1], axis=0)
    key_part = both_win[:, :local_heads]
    value_part = both_win[:, local_heads:]
    row_count = key_part.shape[0]
    key_first = query_first - (window - 1) * tok_count
    key_pos = key_first + jnp.arange(row_count, dtype=jnp.int32)
    seg_padded = jnp.concatenate(
        [jnp.full(((window - 1) * tok_count,), -1, jnp.int32), segment_ids]
    )
    key_seg = lax.dynamic_slice_in_dim(seg_padded, query_first, row_count)
    scores = (
        jnp.einsum("qhd,khd->qhk", queries, key_part, preferred_element_type=jnp.float32) * inv_root
    )
    allowed = (query_seg[:, None] == key_seg[None, :]) & (
        key_pos[None, :] <= query_pos[:, None]
    )
    scores = jnp.where(allowed[:, None, :], scores, -1e30)
    new_max = jnp.maximum(run_max, jnp.max(scores, axis=2))
    weights = jnp.where(allowed[:, None, :], jnp.exp(scores - new_max[:, :, None]), 0.0)
    new_sum = jnp.sum(weights, axis=2)
    probs = weights.astype(jnp.bfloat16)
    new_acc = jnp.einsum("qhk,khd->qhd", probs, value_part, preferred_element_type=jnp.float32)
    attended = (
        (new_acc / new_sum[:, :, None])
        .astype(jnp.bfloat16)
        .reshape(tok_count, local_heads * head_width)
    )
    z_count, y_count = lax.axis_size("zh"), lax.axis_size("y")
    out_flat = out_proj.reshape(local_heads * head_width, z_count, y_count, -1)
    partial_mix = jnp.einsum(
        "tk,kzyc->zytc", attended, out_flat, preferred_element_type=jnp.float32
    )
    col_count = width // hid_count
    col_first = hid_index * col_count
    y_index = lax.axis_index("y")
    got = lax.all_to_all(partial_mix.astype(jnp.bfloat16), "y", split_axis=1, concat_axis=1, tiled=True)
    half = jnp.sum(got.astype(jnp.float32), axis=1).astype(jnp.bfloat16)
    spread = jnp.broadcast_to(half[None], (z_count,) + half.shape)
    got = lax.all_to_all(spread, "zh", split_axis=0, concat_axis=0, tiled=True)
    stream_y = lax.dynamic_index_in_dim(
        stream.reshape(tok_count, z_count, y_count, col_count), y_index, 2, keepdims=False
    ).transpose(1, 0, 2)
    mixed_y = stream_y.astype(jnp.float32) + jnp.sum(got.astype(jnp.float32), axis=0)
    mixed_cols = lax.dynamic_index_in_dim(mixed_y, lax.axis_index("zh"), 0, keepdims=False)
    spread = jnp.broadcast_to(mixed_y.astype(jnp.bfloat16)[None], (y_count,) + mixed_y.shape)
    got = lax.all_to_all(spread, "y", split_axis=0, concat_axis=0, tiled=True)
    mixed_all = got.transpose(2, 1, 0, 3).reshape(tok_count, width).astype(jnp.float32)
    mean_square = jnp.mean(mixed_all * mixed_all, axis=1, keepdims=True)
    normed = (mixed_all * lax.rsqrt(mean_square + 1e-06) * norm_gain).astype(jnp.bfloat16)
    shared_gate_val = jnp.einsum(
        "td,fd->tf", normed, shared_gate, preferred_element_type=jnp.float32
    )
    shared_up_val = jnp.einsum("td,fd->tf", normed, shared_up, preferred_element_type=jnp.float32)
    shared_act = (jax.nn.silu(shared_gate_val) * shared_up_val).astype(jnp.bfloat16)
    shared_part = jnp.einsum(
        "tf,fzyc->zytc",
        shared_act,
        shared_down.reshape(shared_down.shape[0], z_count, y_count, col_count),
        preferred_element_type=jnp.float32,
    ).astype(jnp.bfloat16)
    unit_rows = gate_proj.shape[0]
    held_count = max(1, unit_rows // FF)
    held_units = unit_rows // held_count
    local_experts = EXPERTS // seq_count
    first_local = hid_index * unit_rows // FF
    flat_ids = expert_ids.reshape(-1)
    slot_rank = route_ranks(flat_ids)
    owner_group = flat_ids // local_experts
    local_expert = flat_ids % local_experts
    held_offset = local_expert - first_local
    is_held = (held_offset >= 0) & (held_offset < held_count)
    slot_total = seq_count * held_count * CAP
    send_index = jnp.where(
        is_held, (owner_group * held_count + held_offset) * CAP + slot_rank, slot_total
    )
    slot_ids = jnp.arange(slot_total, dtype=jnp.int32)
    picks = jnp.any(
        send_index.reshape(tok_count, TOP)[None, :, :] == slot_ids[:, None, None], axis=2
    ).astype(jnp.bfloat16)
    send_rows = jnp.dot(picks, normed, preferred_element_type=jnp.float32).astype(jnp.bfloat16)
    send_rows = send_rows.reshape(seq_count, held_count, CAP, width)
    received = lax.all_to_all(send_rows, "seq", split_axis=0, concat_axis=0, tiled=True)
    gate_local = gate_proj.reshape(held_count, held_units, width)
    up_local = up_proj.reshape(held_count, held_units, width)
    down_local = down_proj.reshape(held_count, held_units, z_count, y_count, col_count)
    gate_val = jnp.einsum(
        "sicd,ifd->sicf", received, gate_local, preferred_element_type=jnp.float32
    )
    up_val = jnp.einsum("sicd,ifd->sicf", received, up_local, preferred_element_type=jnp.float32)
    expert_act = (jax.nn.silu(gate_val) * up_val).astype(jnp.bfloat16)
    down_part = jnp.einsum(
        "sicf,ifzyx->zyscx", expert_act, down_local, preferred_element_type=jnp.float32
    ).astype(jnp.bfloat16)
    down_part = down_part.reshape(z_count, y_count, seq_count * CAP, col_count)
    expert_out, shared_out = hid_reduce_pair(down_part, shared_part)
    returned = lax.all_to_all(
        expert_out.reshape(local_experts, seq_count, CAP, col_count),
        "seq",
        split_axis=1,
        concat_axis=1,
        tiled=True,
    ).reshape(-1, col_count)
    pick_index = local_expert * (seq_count * CAP) + owner_group * CAP + slot_rank
    row_ids = jnp.arange(returned.shape[0], dtype=jnp.int32)
    hits = pick_index.reshape(tok_count, TOP)[:, :, None] == row_ids[None, None, :]
    weights = jnp.sum(jnp.where(hits, route_gates[:, :, None], 0.0), axis=1)
    weights_hi = weights.astype(jnp.bfloat16)
    weights_lo = (weights - weights_hi.astype(jnp.float32)).astype(jnp.bfloat16)
    routed_sum = jnp.dot(weights_hi, returned, preferred_element_type=jnp.float32) + jnp.dot(
        weights_lo, returned, preferred_element_type=jnp.float32
    )
    return (mixed_cols + shared_out + routed_sum).astype(jnp.bfloat16)


def solution(mesh):
    y_count = 4
    split_mesh = Mesh(
        mesh.devices.reshape(mesh.shape["seq"], mesh.shape["hid"] // y_count, y_count),
        ("seq", "zh", "y"),
    )
    hid = ("zh", "y")
    placed = (
        P("seq", None),
        P("seq", hid, None),
        P("seq", hid, None),
        P("seq", hid, None),
        P(),
        P(hid, None, None),
        P(),
        P("seq", None),
        P("seq", None),
        P(("seq",) + hid, None),
        P(("seq",) + hid, None),
        P(("seq",) + hid, None),
        P(hid, None),
        P(hid, None),
        P(hid, None),
    )
    return jax.shard_map(
        on_device, mesh=split_mesh, in_specs=placed, out_specs=P("seq", hid), check_vma=False
    )
```

```python
import jax
import jax.numpy as jnp
from jax import lax
from jax.sharding import Mesh, PartitionSpec as P

EXPERTS = 64
FF = 1408
TOP = 6
CAP = 64
LONGEST = 4096


def seq_gather(rows, seq_count):
    spread = jnp.broadcast_to(rows[None], (seq_count,) + rows.shape)
    got = lax.all_to_all(spread, "seq", split_axis=0, concat_axis=0, tiled=True)
    return got.reshape((seq_count * rows.shape[0],) + rows.shape[1:])


def hid_scatter_sum(part):
    got = lax.all_to_all(part, "y", split_axis=1, concat_axis=1, tiled=True)
    half = jnp.sum(got.astype(jnp.float32), axis=1).astype(jnp.bfloat16)
    got = lax.all_to_all(half, "zh", split_axis=0, concat_axis=0, tiled=True)
    return jnp.sum(got.astype(jnp.float32), axis=0)


def hid_reduce_pair(routed, shared):
    routed_rows = routed.shape[2]
    both = jnp.concatenate([routed, shared], axis=2)
    got = lax.all_to_all(both, "y", split_axis=1, concat_axis=1, tiled=True)
    half = jnp.sum(got.astype(jnp.float32), axis=1).astype(jnp.bfloat16)
    got = lax.all_to_all(half, "zh", split_axis=0, concat_axis=0, tiled=True)
    shared_sum = jnp.sum(got[:, routed_rows:].astype(jnp.float32), axis=0)
    return got[:, :routed_rows], shared_sum


def hid_gather(cols):
    rows, col_count = cols.shape
    z_count, y_count = lax.axis_size("zh"), lax.axis_size("y")
    spread = jnp.broadcast_to(cols[:, None, :], (rows, z_count, col_count))
    got = lax.all_to_all(spread, "zh", split_axis=1, concat_axis=1, tiled=True)
    spread = jnp.broadcast_to(got[:, :, None, :], (rows, z_count, y_count, col_count))
    got = lax.all_to_all(spread, "y", split_axis=2, concat_axis=2, tiled=True)
    return got.reshape(rows, z_count * y_count * col_count)


def route_ranks(flat_ids):
    span = 64
    blocks = flat_ids.shape[0] // span
    onehot = (flat_ids[:, None] == jnp.arange(EXPERTS, dtype=jnp.int32)[None, :]).astype(
        jnp.bfloat16
    )
    onehot = onehot.reshape(blocks, span, EXPERTS)
    lower = jnp.arange(span)[:, None] >= jnp.arange(span)[None, :]
    within = jnp.einsum(
        "ij,bjk->bik", lower.astype(jnp.bfloat16), onehot, preferred_element_type=jnp.float32
    )
    earlier = jnp.arange(blocks)[:, None] > jnp.arange(blocks)[None, :]
    before = jnp.dot(
        earlier.astype(jnp.bfloat16),
        within[:, -1, :].astype(jnp.bfloat16),
        preferred_element_type=jnp.float32,
    )
    counts = within + before[:, None, :]
    ranks = jnp.sum(counts * onehot.astype(jnp.float32), axis=2) - 1.0
    return ranks.astype(jnp.int32).reshape(-1)


def on_device(
    stream,
    queries,
    key_rows,
    value_rows,
    segment_ids,
    out_proj,
    norm_gain,
    expert_ids,
    route_gates,
    gate_proj,
    up_proj,
    down_proj,
    shared_gate,
    shared_up,
    shared_down,
):
    tok_count = queries.shape[0]
    local_heads = queries.shape[1]
    head_width = queries.shape[2]
    width = stream.shape[1]
    inv_root = head_width ** (-0.5)
    seq_count = lax.axis_size("seq")
    hid_count = lax.axis_size("zh") * lax.axis_size("y")
    hid_index = lax.axis_index("zh") * lax.axis_size("y") + lax.axis_index("y")
    query_first = lax.axis_index("seq") * tok_count
    query_seg = lax.dynamic_slice_in_dim(segment_ids, query_first, tok_count)
    query_pos = query_first + jnp.arange(tok_count, dtype=jnp.int32)
    run_max = jnp.full((tok_count, local_heads), -1e30, jnp.float32)
    window = min(seq_count, -(-LONGEST // tok_count) + 1)
    both = jnp.concatenate([key_rows, value_rows], axis=1)
    blocks = [both]
    for shift in range(1, window):
        pairs = [(i, i + shift) for i in range(seq_count - shift)]
        blocks.append(lax.ppermute(both, "seq", pairs))
    both_win = jnp.concatenate(blocks[::-1], axis=0)
    key_part = both_win[:, :local_heads]
    value_part = both_win[:, local_heads:]
    row_count = key_part.shape[0]
    key_first = query_first - (window - 1) * tok_count
    key_pos = key_first + jnp.arange(row_count, dtype=jnp.int32)
    seg_padded = jnp.concatenate(
        [jnp.full(((window - 1) * tok_count,), -1, jnp.int32), segment_ids]
    )
    key_seg = lax.dynamic_slice_in_dim(seg_padded, query_first, row_count)
    scores = (
        jnp.einsum("qhd,khd->qhk", queries, key_part, preferred_element_type=jnp.float32) * inv_root
    )
    allowed = (query_seg[:, None] == key_seg[None, :]) & (
        key_pos[None, :] <= query_pos[:, None]
    )
    scores = jnp.where(allowed[:, None, :], scores, -1e30)
    new_max = jnp.maximum(run_max, jnp.max(scores, axis=2))
    weights = jnp.where(allowed[:, None, :], jnp.exp(scores - new_max[:, :, None]), 0.0)
    new_sum = jnp.sum(weights, axis=2)
    probs = weights.astype(jnp.bfloat16)
    new_acc = jnp.einsum("qhk,khd->qhd", probs, value_part, preferred_element_type=jnp.float32)
    attended = (
        (new_acc / new_sum[:, :, None])
        .astype(jnp.bfloat16)
        .reshape(tok_count, local_heads * head_width)
    )
    z_count, y_count = lax.axis_size("zh"), lax.axis_size("y")
    out_flat = out_proj.reshape(local_heads * head_width, z_count, y_count, -1)
    partial_mix = jnp.einsum(
        "tk,kzyc->zytc", attended, out_flat, preferred_element_type=jnp.float32
    )
    col_count = width // hid_count
    col_first = hid_index * col_count
    mixed_cols = lax.dynamic_slice_in_dim(stream, col_first, col_count, 1).astype(
        jnp.float32
    ) + hid_scatter_sum(partial_mix.astype(jnp.bfloat16))
    mixed_all = hid_gather(mixed_cols.astype(jnp.bfloat16)).astype(jnp.float32)
    mean_square = jnp.mean(mixed_all * mixed_all, axis=1, keepdims=True)
    normed = (mixed_all * lax.rsqrt(mean_square + 1e-06) * norm_gain).astype(jnp.bfloat16)
    shared_gate_val = jnp.einsum(
        "td,fd->tf", normed, shared_gate, preferred_element_type=jnp.float32
    )
    shared_up_val = jnp.einsum("td,fd->tf", normed, shared_up, preferred_element_type=jnp.float32)
    shared_act = (jax.nn.silu(shared_gate_val) * shared_up_val).astype(jnp.bfloat16)
    shared_part = jnp.einsum(
        "tf,fzyc->zytc",
        shared_act,
        shared_down.reshape(shared_down.shape[0], z_count, y_count, col_count),
        preferred_element_type=jnp.float32,
    ).astype(jnp.bfloat16)
    unit_rows = gate_proj.shape[0]
    held_count = max(1, unit_rows // FF)
    held_units = unit_rows // held_count
    local_experts = EXPERTS // seq_count
    first_local = hid_index * unit_rows // FF
    flat_ids = expert_ids.reshape(-1)
    slot_rank = route_ranks(flat_ids)
    owner_group = flat_ids // local_experts
    local_expert = flat_ids % local_experts
    held_offset = local_expert - first_local
    is_held = (held_offset >= 0) & (held_offset < held_count)
    slot_total = seq_count * held_count * CAP
    send_index = jnp.where(
        is_held, (owner_group * held_count + held_offset) * CAP + slot_rank, slot_total
    )
    slot_ids = jnp.arange(slot_total, dtype=jnp.int32)
    picks = jnp.any(
        send_index.reshape(tok_count, TOP)[None, :, :] == slot_ids[:, None, None], axis=2
    ).astype(jnp.bfloat16)
    send_rows = jnp.dot(picks, normed, preferred_element_type=jnp.float32).astype(jnp.bfloat16)
    send_rows = send_rows.reshape(seq_count, held_count, CAP, width)
    received = lax.all_to_all(send_rows, "seq", split_axis=0, concat_axis=0, tiled=True)
    gate_local = gate_proj.reshape(held_count, held_units, width)
    up_local = up_proj.reshape(held_count, held_units, width)
    down_local = down_proj.reshape(held_count, held_units, z_count, y_count, col_count)
    gate_val = jnp.einsum(
        "sicd,ifd->sicf", received, gate_local, preferred_element_type=jnp.float32
    )
    up_val = jnp.einsum("sicd,ifd->sicf", received, up_local, preferred_element_type=jnp.float32)
    expert_act = (jax.nn.silu(gate_val) * up_val).astype(jnp.bfloat16)
    down_part = jnp.einsum(
        "sicf,ifzyx->zyscx", expert_act, down_local, preferred_element_type=jnp.float32
    ).astype(jnp.bfloat16)
    down_part = down_part.reshape(z_count, y_count, seq_count * CAP, col_count)
    expert_out, shared_out = hid_reduce_pair(down_part, shared_part)
    returned = lax.all_to_all(
        expert_out.reshape(local_experts, seq_count, CAP, col_count),
        "seq",
        split_axis=1,
        concat_axis=1,
        tiled=True,
    ).reshape(-1, col_count)
    pick_index = local_expert * (seq_count * CAP) + owner_group * CAP + slot_rank
    row_ids = jnp.arange(returned.shape[0], dtype=jnp.int32)
    hits = pick_index.reshape(tok_count, TOP)[:, :, None] == row_ids[None, None, :]
    weights = jnp.sum(jnp.where(hits, route_gates[:, :, None], 0.0), axis=1)
    routed_sum = jnp.dot(
        weights,
        returned.astype(jnp.float32),
        precision=lax.Precision.HIGHEST,
        preferred_element_type=jnp.float32,
    )
    return (mixed_cols + shared_out + routed_sum).astype(jnp.bfloat16)


def solution(mesh):
    y_count = 4
    split_mesh = Mesh(
        mesh.devices.reshape(mesh.shape["seq"], mesh.shape["hid"] // y_count, y_count),
        ("seq", "zh", "y"),
    )
    hid = ("zh", "y")
    placed = (
        P("seq", None),
        P("seq", hid, None),
        P("seq", hid, None),
        P("seq", hid, None),
        P(),
        P(hid, None, None),
        P(),
        P("seq", None),
        P("seq", None),
        P(("seq",) + hid, None),
        P(("seq",) + hid, None),
        P(("seq",) + hid, None),
        P(hid, None),
        P(hid, None),
        P(hid, None),
    )
    return jax.shard_map(
        on_device, mesh=split_mesh, in_specs=placed, out_specs=P("seq", hid), check_vma=False
    )
```
